512 devices in a mesh: tm: 32 (over x, y), space: 16 (over z, core).
Axes of the slice: x: 4, y: 8, z: 8, core: 2. Of those that a mesh axis runs over, the one named last changes fastest.
Arguments:
- data: bfloat16 [4096, 131072], P('tm', 'space'), may hold values from -40 to 40
- weights: float32 [131072], P('space'), may hold values from 1 to 30
- freqs: int32 [32], replicated, may hold values from 0 to 32, as said below
- n_keep: int32 [32], replicated, may hold values from 1 to 64, as said below
Outputs:
- mode_field: bfloat16 [32, 2, 64, 131072], P('tm', None, None, 'space')
- energy: float32 [32], P('tm')
The draws below stay inside these ranges and needn't reach their ends.
Inputs may be any that keep to these rules, and one draw needn't show every extreme that they name: `freqs`: 32 distinct bins, among them 0 and 32, in an order drawn from the seed. `n_keep`: some frequency keeps all 64 columns and another keeps one.
All inputs are finite; a program needn't handle non-finite values.
Results may differ from the reference program's by a relative error of at most 0.0052.
Values may be sent and summed in bfloat16 or wider, within the bound.
No kernel may reach another device: no remote copies, remote signals or barrier semaphores. Data moves between devices by JAX's collectives and lax.ppermute only.
A program may use at most 64 MiB of HBM per device.

```python
import jax
import jax.numpy as jnp
from jax import lax

NT = 64
P_DEV = 8192
NS_STEPS = 4
BLOCKS = 64
NF = 32
POINTS = 131072


def draw_data(key, part):
    subkeys = jax.random.split(key, 9)
    regions = POINTS // P_DEV
    shape_four = (BLOCKS, NT, regions, P_DEV)
    noise_part = jnp.clip(jax.random.normal(subkeys[0], shape_four, jnp.float32), -5.0, 5.0)
    amplitude = jnp.exp(jax.random.uniform(subkeys[1], (regions, P_DEV), jnp.float32, jnp.log(0.3), jnp.log(3.0)))
    tone_bins = jax.random.randint(subkeys[2], (regions, P_DEV), 0, NT // 2 + 1)
    tone_phase = jax.random.uniform(subkeys[3], (regions, P_DEV), jnp.float32, -jnp.pi, jnp.pi)
    block_scale = jnp.exp(jax.random.uniform(subkeys[4], (BLOCKS, regions), jnp.float32, jnp.log(0.5), jnp.log(2.0)))
    region_drift = jax.random.uniform(subkeys[6], (regions, 1), jnp.float32, 0.05, 0.45)
    drift = region_drift + jax.random.uniform(subkeys[7], (regions, P_DEV), jnp.float32, -0.05, 0.05)
    strength = jnp.exp(jax.random.uniform(subkeys[8], (regions, 1), jnp.float32, jnp.log(0.5), jnp.log(2.5)))
    time_int = jnp.arange(NT, dtype=jnp.int32)
    block_float = jnp.arange(BLOCKS, dtype=jnp.int32).astype(jnp.float32)
    wrapped = time_int[:, None, None] * tone_bins[None, :, :] % NT
    grid_phase = 2.0 * jnp.pi * wrapped.astype(jnp.float32) / NT
    block_time = block_float[:, None] + time_int.astype(jnp.float32)[None, :] / NT
    drift_phase = 2.0 * jnp.pi * drift[None, None, :, :] * block_time[:, :, None, None]
    tone_part = jnp.cos(grid_phase[None] + drift_phase + tone_phase[None, None])
    noisy = noise_part * block_scale[:, None, :, None]
    values = amplitude[None, None] * (noisy + strength[None, None] * tone_part)
    return values.reshape(BLOCKS * NT, POINTS).astype(jnp.bfloat16)


def draw_weights(key, part):
    base = jnp.exp(jax.random.uniform(key, (POINTS,), jnp.float32, 0.0, jnp.log(10.0)))
    ramp = 1.0 + 2.0 * jnp.arange(POINTS, dtype=jnp.float32) / (POINTS - 1)
    return base * ramp


def draw_freqs(key, part):
    inner = jax.random.permutation(jax.random.fold_in(key, 11), NT // 2 - 1).astype(jnp.int32) + 1
    chosen = inner[:NF - 2]
    full_list = jnp.concatenate([jnp.zeros((1,), jnp.int32), chosen, jnp.full((1,), NT // 2, jnp.int32)])
    shuffle = jax.random.permutation(jax.random.fold_in(key, 12), NF)
    return full_list[shuffle]


def draw_n_keep(key, part):
    counts_drawn = jax.random.randint(jax.random.fold_in(key, 21), (NF,), 1, BLOCKS + 1)
    forced_at = jax.random.randint(jax.random.fold_in(key, 22), (), 0, NF)
    positions = jnp.arange(NF, dtype=jnp.int32)
    counts_drawn = jnp.where(positions == forced_at, BLOCKS, counts_drawn)
    counts_drawn = jnp.where(positions == (forced_at + 1) % NF, 1, counts_drawn)
    return counts_drawn.astype(jnp.int32)


def setup_inputs(seed: int = 0) -> dict:
    streams_of = jax.random.split(jax.random.key(seed), 5)
    data = draw_data(jax.random.fold_in(streams_of[4], 71), 0)
    weights = draw_weights(jax.random.fold_in(streams_of[4], 71), 0)
    freqs = draw_freqs(jax.random.fold_in(streams_of[4], 71), 0)
    n_keep = draw_n_keep(jax.random.fold_in(streams_of[4], 71), 0)
    return {"data": data, "weights": weights, "freqs": freqs, "n_keep": n_keep}


def spectra_table(freqs):
    time_int = jnp.arange(NT, dtype=jnp.int32)
    time_float = time_int.astype(jnp.float32)
    window = 0.5 - 0.5 * jnp.cos(2.0 * jnp.pi * time_float / NT)
    norm = jnp.sqrt(jnp.sum(window * window))
    wrapped = freqs[:, None] * time_int[None, :] % NT
    phase_angle = 2.0 * jnp.pi * wrapped.astype(jnp.float32) / NT
    real_rows = window[None, :] * jnp.cos(phase_angle) / norm
    imag_rows = -window[None, :] * jnp.sin(phase_angle) / norm
    return jnp.concatenate([real_rows, imag_rows], axis=0).astype(jnp.bfloat16)

def inverse_root(embedded):
    size_two = embedded.shape[0]
    frobenius = jnp.sqrt(jnp.sum(embedded * embedded) + 1e-06)
    identity = jnp.eye(size_two, dtype=jnp.float32)
    current = embedded / frobenius
    result = identity
    for sweep in range(NS_STEPS):
        factor = 1.5 * identity - 0.5 * jnp.dot(result, current, precision=lax.Precision.HIGHEST)
        current = jnp.dot(current, factor, precision=lax.Precision.HIGHEST)
        result = jnp.dot(factor, result, precision=lax.Precision.HIGHEST)
    return result

def reference(data, weights, freqs, n_keep):
    dft_table = spectra_table(freqs)
    block_view = data.reshape(BLOCKS, NT, POINTS)

    def one_freq(position):
        table_rows = jnp.stack([lax.dynamic_index_in_dim(dft_table, position, 0, keepdims=False), lax.dynamic_index_in_dim(dft_table, position + NF, 0, keepdims=False)])
        spectra = lax.map(lambda block_data: jnp.dot(table_rows, block_data, preferred_element_type=jnp.float32), block_view)
        spectra_re = spectra[:, 0]
        spectra_im = spectra[:, 1]
        stacked = jnp.concatenate([spectra_re, spectra_im], axis=0)
        square = jnp.dot(stacked * weights[None, :], stacked.T, precision=lax.Precision.HIGHEST) / POINTS
        g_one = square[:BLOCKS, :BLOCKS] + square[BLOCKS:, BLOCKS:]
        g_two = square[:BLOCKS, BLOCKS:] - square[BLOCKS:, :BLOCKS]
        embedded = jnp.concatenate([jnp.concatenate([g_one, -g_two], axis=1), jnp.concatenate([g_two, g_one], axis=1)], axis=0)
        inv_root = inverse_root(embedded)
        z_top = inv_root[:BLOCKS, :BLOCKS]
        z_low = inv_root[BLOCKS:, :BLOCKS]
        mode_re = jnp.dot(z_top.T, spectra_re, precision=lax.Precision.HIGHEST) - jnp.dot(z_low.T, spectra_im, precision=lax.Precision.HIGHEST)
        mode_im = jnp.dot(z_top.T, spectra_im, precision=lax.Precision.HIGHEST) + jnp.dot(z_low.T, spectra_re, precision=lax.Precision.HIGHEST)
        kept_count = lax.dynamic_index_in_dim(n_keep, position, 0, keepdims=False)
        kept_mask = (jnp.arange(BLOCKS, dtype=jnp.int32) < kept_count)[:, None]
        both_parts = jnp.stack([mode_re, mode_im])
        mode_field = jnp.where(kept_mask, both_parts, jnp.zeros_like(both_parts)).astype(jnp.bfloat16)
        energy = jnp.trace(g_one) / BLOCKS
        return (mode_field, energy)
    mode_field, energy = lax.map(one_freq, jnp.arange(NF, dtype=jnp.int32))
    return (mode_field, energy)
```

```python
import jax
import jax.numpy as jnp
from jax import lax
from jax.sharding import PartitionSpec as P

NT = 64
NS_STEPS = 4
HIGH = lax.Precision.HIGHEST


def spectra_table(freqs):
    time_int = jnp.arange(NT, dtype=jnp.int32)
    time_float = time_int.astype(jnp.float32)
    window = 0.5 - 0.5 * jnp.cos(2.0 * jnp.pi * time_float / NT)
    norm = jnp.sqrt(jnp.sum(window * window))
    wrapped = freqs[:, None] * time_int[None, :] % NT
    phase_angle = 2.0 * jnp.pi * wrapped.astype(jnp.float32) / NT
    real_rows = window[None, :] * jnp.cos(phase_angle) / norm
    imag_rows = -window[None, :] * jnp.sin(phase_angle) / norm
    return jnp.concatenate([real_rows, imag_rows], axis=0).astype(jnp.bfloat16)


def transform_blocks(dft_table, snapshots, freq_count):
    local_blocks = snapshots.shape[0] // NT
    point_count = snapshots.shape[1]
    block_view = snapshots.reshape(local_blocks, NT, point_count)
    table_view = dft_table.reshape(2, freq_count, NT)
    return jnp.einsum(
        "rft,btp->frbp", table_view, block_view, preferred_element_type=jnp.float32
    )


def butterfly_sum(value, axis, size):
    step = 1
    while step < size:
        pairs = [(i, i ^ step) for i in range(size)]
        value = value + lax.ppermute(value, axis, pairs)
        step *= 2
    return value


def inverse_root(embedded):
    size_two = embedded.shape[0]
    frobenius = jnp.sqrt(jnp.sum(embedded * embedded) + 1e-06)
    identity = jnp.eye(size_two, dtype=jnp.float32)
    current = embedded / frobenius
    result = identity
    for sweep in range(NS_STEPS):
        factor = 1.5 * identity - 0.5 * jnp.dot(result, current, precision=HIGH)
        current = jnp.dot(current, factor, precision=HIGH)
        result = jnp.dot(factor, result, precision=HIGH)
    return result


def shards(data, weights, freqs, n_keep):
    tm_count = lax.axis_size("tm")
    space_count = lax.axis_size("space")
    freq_count = freqs.shape[0]
    points_here = data.shape[1]
    total_points = points_here * space_count
    local_blocks = data.shape[0] // NT
    block_count = local_blocks * tm_count
    rows = 2 * block_count

    dft_table = spectra_table(freqs)
    spectra = transform_blocks(dft_table, data, freq_count)
    gathered = lax.all_to_all(spectra, "tm", split_axis=0, concat_axis=0, tiled=True)
    stacked = gathered.reshape(rows, points_here)

    square = jnp.dot(stacked * weights[None, :], stacked.T, precision=HIGH) / total_points
    square = square.reshape(tm_count, 2, local_blocks, tm_count, 2, local_blocks)
    square = square.transpose(1, 0, 2, 4, 3, 5).reshape(rows, rows)
    g_one = square[:block_count, :block_count] + square[block_count:, block_count:]
    g_two = square[:block_count, block_count:] - square[block_count:, :block_count]
    summed = butterfly_sum(jnp.stack([g_one, g_two]), "space", space_count)
    g_one = summed[0]
    g_two = summed[1]

    embedded = jnp.concatenate(
        [jnp.concatenate([g_one, -g_two], axis=1), jnp.concatenate([g_two, g_one], axis=1)], axis=0
    )
    inv_root = inverse_root(embedded)
    z_top = inv_root[:block_count, :block_count]
    z_low = inv_root[block_count:, :block_count]
    coeff = jnp.concatenate(
        [jnp.concatenate([z_top.T, -z_low.T], axis=1), jnp.concatenate([z_low.T, z_top.T], axis=1)],
        axis=0,
    )
    coeff = coeff.reshape(rows, 2, tm_count, local_blocks).transpose(0, 2, 1, 3).reshape(rows, rows)
    modes = jnp.dot(coeff, stacked, precision=HIGH).reshape(1, 2, block_count, points_here)

    kept_count = lax.dynamic_slice_in_dim(n_keep, lax.axis_index("tm"), 1)
    kept_mask = jnp.arange(block_count, dtype=jnp.int32)[None, None, :, None] < kept_count[:, None, None, None]
    mode_field = jnp.where(kept_mask, modes, jnp.zeros_like(modes)).astype(jnp.bfloat16)
    energy = (jnp.trace(g_one) / block_count).reshape(1)
    return (mode_field, energy)


def solution(mesh):
    placed = (P("tm", "space"), P("space"), P(), P())
    return jax.shard_map(
        shards,
        mesh=mesh,
        in_specs=placed,
        out_specs=(P("tm", None, None, "space"), P("tm")),
        check_vma=False,
    )
```

```python
import jax
import jax.numpy as jnp
from jax import lax
from jax.sharding import PartitionSpec as P

NT = 64
NS_STEPS = 4
HIGH = lax.Precision.HIGHEST
THREE_PASS = lax.Precision.HIGH
LINK_SCALE = 128.0


def spectra_table(freqs):
    time_int = jnp.arange(NT, dtype=jnp.int32)
    time_float = time_int.astype(jnp.float32)
    window = 0.5 - 0.5 * jnp.cos(2.0 * jnp.pi * time_float / NT)
    norm = jnp.sqrt(jnp.sum(window * window))
    wrapped = freqs[:, None] * time_int[None, :] % NT
    phase_angle = 2.0 * jnp.pi * wrapped.astype(jnp.float32) / NT
    real_rows = window[None, :] * jnp.cos(phase_angle) / norm
    imag_rows = -window[None, :] * jnp.sin(phase_angle) / norm
    return jnp.concatenate([real_rows, imag_rows], axis=0).astype(jnp.bfloat16)


def transform_blocks(dft_table, snapshots, freq_count):
    local_blocks = snapshots.shape[0] // NT
    point_count = snapshots.shape[1]
    block_view = snapshots.reshape(local_blocks, NT, point_count)
    table_view = dft_table.reshape(2, freq_count, NT)
    return jnp.einsum(
        "rft,btp->frbp", table_view, block_view, preferred_element_type=jnp.float32
    )


def butterfly_sum(value, axis, size):
    step = 1
    while step < size:
        pairs = [(i, i ^ step) for i in range(size)]
        value = value + lax.ppermute(value, axis, pairs)
        step *= 2
    return value


def inverse_root(embedded):
    size_two = embedded.shape[0]
    frobenius = jnp.sqrt(jnp.sum(embedded * embedded) + 1e-06)
    identity = jnp.eye(size_two, dtype=jnp.float32)
    current = embedded / frobenius
    result = identity
    for sweep in range(NS_STEPS):
        factor = 1.5 * identity - 0.5 * jnp.dot(result, current, precision=HIGH)
        current = jnp.dot(current, factor, precision=HIGH)
        result = jnp.dot(factor, result, precision=HIGH)
    return result


def shards(data, weights, freqs, n_keep):
    tm_count = lax.axis_size("tm")
    space_count = lax.axis_size("space")
    freq_count = freqs.shape[0]
    points_here = data.shape[1]
    total_points = points_here * space_count
    local_blocks = data.shape[0] // NT
    block_count = local_blocks * tm_count
    rows = 2 * block_count

    dft_table = spectra_table(freqs)
    spectra = transform_blocks(dft_table, data, freq_count)
    sent = (spectra * LINK_SCALE).astype(jnp.float16)
    gathered = lax.all_to_all(sent, "tm", split_axis=0, concat_axis=0, tiled=True)
    stacked = gathered.reshape(rows, points_here).astype(jnp.float32) * (1.0 / LINK_SCALE)

    square = jnp.dot(stacked * weights[None, :], stacked.T, precision=THREE_PASS) / total_points
    square = square.reshape(tm_count, 2, local_blocks, tm_count, 2, local_blocks)
    square = square.transpose(1, 0, 2, 4, 3, 5).reshape(rows, rows)
    g_one = square[:block_count, :block_count] + square[block_count:, block_count:]
    g_two = square[:block_count, block_count:] - square[block_count:, :block_count]
    summed = butterfly_sum(jnp.stack([g_one, g_two]), "space", space_count)
    g_one = summed[0]
    g_two = summed[1]

    embedded = jnp.concatenate(
        [jnp.concatenate([g_one, -g_two], axis=1), jnp.concatenate([g_two, g_one], axis=1)], axis=0
    )
    inv_root = inverse_root(embedded)
    z_top = inv_root[:block_count, :block_count]
    z_low = inv_root[block_count:, :block_count]
    coeff = jnp.concatenate(
        [jnp.concatenate([z_top.T, -z_low.T], axis=1), jnp.concatenate([z_low.T, z_top.T], axis=1)],
        axis=0,
    )
    coeff = coeff.reshape(rows, 2, tm_count, local_blocks).transpose(0, 2, 1, 3).reshape(rows, rows)
    modes = jnp.dot(coeff, stacked, precision=THREE_PASS).reshape(1, 2, block_count, points_here)

    kept_count = lax.dynamic_slice_in_dim(n_keep, lax.axis_index("tm"), 1)
    kept_mask = jnp.arange(block_count, dtype=jnp.int32)[None, None, :, None] < kept_count[:, None, None, None]
    mode_field = jnp.where(kept_mask, modes, jnp.zeros_like(modes)).astype(jnp.bfloat16)
    energy = (jnp.trace(g_one) / block_count).reshape(1)
    return (mode_field, energy)


def solution(mesh):
    placed = (P("tm", "space"), P("space"), P(), P())
    return jax.shard_map(
        shards,
        mesh=mesh,
        in_specs=placed,
        out_specs=(P("tm", None, None, "space"), P("tm")),
        check_vma=False,
    )
```

```python
import jax
import jax.numpy as jnp
from jax import lax
from jax.sharding import PartitionSpec as P
from jax.experimental import pallas as pl
from jax.experimental.pallas import tpu as pltpu

NT = 64
NS_STEPS = 4
HIGH = lax.Precision.HIGHEST
LINK_SCALE = 128.0


def spectra_table(freqs):
    time_int = jnp.arange(NT, dtype=jnp.int32)
    time_float = time_int.astype(jnp.float32)
    window = 0.5 - 0.5 * jnp.cos(2.0 * jnp.pi * time_float / NT)
    norm = jnp.sqrt(jnp.sum(window * window))
    wrapped = freqs[:, None] * time_int[None, :] % NT
    phase_angle = 2.0 * jnp.pi * wrapped.astype(jnp.float32) / NT
    real_rows = window[None, :] * jnp.cos(phase_angle) / norm
    imag_rows = -window[None, :] * jnp.sin(phase_angle) / norm
    return jnp.concatenate([real_rows, imag_rows], axis=0).astype(jnp.bfloat16)


def transform_blocks(dft_table, snapshots, freq_count, halves):
    local_blocks = snapshots.shape[0] // NT
    points = snapshots.shape[1]
    table_view = dft_table.reshape(2, freq_count, NT).transpose(1, 0, 2)
    chooser = jnp.eye(local_blocks, dtype=dft_table.dtype)
    lifted = table_view[:, :, None, None, :] * chooser[None, None, :, :, None]
    lifted = lifted.reshape(freq_count * 2 * local_blocks, local_blocks * NT)
    split_view = snapshots.reshape(local_blocks * NT, halves, points // halves)
    spectra = jnp.einsum("qc,chp->qhp", lifted, split_view, preferred_element_type=jnp.float32)
    return spectra.reshape(freq_count * 2 * local_blocks * halves, points // halves)


def split_pair(value):
    rounded = lax.reduce_precision(value, exponent_bits=8, mantissa_bits=7)
    return rounded.astype(jnp.bfloat16), (value - rounded).astype(jnp.bfloat16)


NT_DIMS = (((1,), (1,)), ((), ()))


def gram_kernel(hi_ref, lo_ref, w_ref, o_ref):
    @pl.when(pl.program_id(0) == 0)
    def _():
        o_ref[...] = jnp.zeros_like(o_ref)

    x_hi = hi_ref[...]
    x_lo = lo_ref[...]
    x = x_hi.astype(jnp.float32) + x_lo.astype(jnp.float32)
    odd = lax.broadcasted_iota(jnp.int32, x.shape, 0) % 2 == 1
    row_weights = jnp.where(odd, w_ref[1:2, :], w_ref[0:1, :])
    y_hi, y_lo = split_pair(x * row_weights)
    acc = lax.dot_general(x_hi, y_hi, NT_DIMS, preferred_element_type=jnp.float32)
    acc += lax.dot_general(x_lo, y_hi, NT_DIMS, preferred_element_type=jnp.float32)
    acc += lax.dot_general(x_hi, y_lo, NT_DIMS, preferred_element_type=jnp.float32)
    o_ref[...] += acc


def gram_call(high, low, weights, chunk):
    rows, points = high.shape
    return pl.pallas_call(
        gram_kernel,
        grid=(points // chunk,),
        in_specs=[
            pl.BlockSpec((rows, chunk), lambda k: (0, k)),
            pl.BlockSpec((rows, chunk), lambda k: (0, k)),
            pl.BlockSpec((2, chunk), lambda k: (0, k)),
        ],
        out_specs=pl.BlockSpec((rows, rows), lambda k: (0, 0)),
        out_shape=jax.ShapeDtypeStruct((rows, rows), jnp.float32),
        cost_estimate=pl.CostEstimate(
            flops=6 * rows * rows * points, transcendentals=0, bytes_accessed=4 * rows * points
        ),
    )(high, low, weights.reshape(2, points))


def mode_kernel(c_hi_ref, c_lo_ref, hi_ref, lo_ref, o_ref):
    x_hi = hi_ref[...]
    x_lo = lo_ref[...]
    c_hi = c_hi_ref[...]
    acc = jnp.dot(c_hi, x_hi, preferred_element_type=jnp.float32)
    acc += jnp.dot(c_lo_ref[...], x_hi, preferred_element_type=jnp.float32)
    acc += jnp.dot(c_hi, x_lo, preferred_element_type=jnp.float32)
    o_ref[...] = acc.astype(o_ref.dtype)


def mode_call(coeff_halves, high, low, chunk):
    halves, out_rows, rows = coeff_halves.shape
    points = high.shape[1]
    steps = points // chunk
    c_hi, c_lo = split_pair(coeff_halves)
    return pl.pallas_call(
        mode_kernel,
        grid=(halves, steps),
        in_specs=[
            pl.BlockSpec((None, out_rows, rows), lambda h, k: (h, 0, 0)),
            pl.BlockSpec((None, out_rows, rows), lambda h, k: (h, 0, 0)),
            pl.BlockSpec((rows, chunk), lambda h, k: (0, k)),
            pl.BlockSpec((rows, chunk), lambda h, k: (0, k)),
        ],
        out_specs=pl.BlockSpec((out_rows, chunk), lambda h, k: (0, h * steps + k)),
        out_shape=jax.ShapeDtypeStruct((out_rows, halves * points), jnp.bfloat16),
        cost_estimate=pl.CostEstimate(
            flops=6 * out_rows * rows * points * halves,
            transcendentals=0,
            bytes_accessed=4 * rows * points * halves + 2 * out_rows * points * halves,
        ),
    )(c_hi, c_lo, high, low)


def butterfly_sum(value, axis, size):
    step = 1
    while step < size:
        pairs = [(i, i ^ step) for i in range(size)]
        value = value + lax.ppermute(value, axis, pairs)
        step *= 2
    return value


def inverse_root(embedded):
    size_two = embedded.shape[0]
    frobenius = jnp.sqrt(jnp.sum(embedded * embedded) + 1e-06)
    identity = jnp.eye(size_two, dtype=jnp.float32)
    current = embedded / frobenius
    result = identity
    for sweep in range(NS_STEPS):
        factor = 1.5 * identity - 0.5 * jnp.dot(result, current, precision=HIGH)
        current = jnp.dot(current, factor, precision=HIGH)
        result = jnp.dot(factor, result, precision=HIGH)
    return result


def shards(data, weights, freqs, n_keep):
    tm_count = lax.axis_size("tm")
    space_count = lax.axis_size("space")
    freq_count = freqs.shape[0]
    points_here = data.shape[1]
    total_points = points_here * space_count
    local_blocks = data.shape[0] // NT
    block_count = local_blocks * tm_count
    rows = 2 * block_count

    dft_table = spectra_table(freqs)
    halves = 2
    spectra = transform_blocks(dft_table, data, freq_count, halves)
    sent = (spectra * LINK_SCALE).astype(jnp.float16)
    received = lax.all_to_all(sent, "tm", split_axis=0, concat_axis=0, tiled=True)
    high, low = split_pair(received.astype(jnp.float32))
    recv_rows = received.shape[0]

    square = gram_call(high, low, weights, 1024) * (1.0 / (LINK_SCALE * LINK_SCALE * total_points))
    natural = jnp.arange(rows, dtype=jnp.int32)
    part, block = natural // block_count, natural % block_count
    home = (block // local_blocks) * (2 * local_blocks * halves) + part * (local_blocks * halves) + (block % local_blocks) * halves
    recv_index = jnp.arange(recv_rows, dtype=jnp.int32)
    pick = [(recv_index[None, :] == (home + h)[:, None]).astype(jnp.float32) for h in range(halves)]
    same_half = recv_index[:, None] % halves == recv_index[None, :] % halves
    either = pick[0] + pick[1]
    square = jnp.where(same_half, square, jnp.zeros_like(square))
    square = jnp.dot(jnp.dot(either, square, precision=HIGH), either.T, precision=HIGH)
    g_one = square[:block_count, :block_count] + square[block_count:, block_count:]
    g_two = square[:block_count, block_count:] - square[block_count:, :block_count]
    summed = butterfly_sum(jnp.stack([g_one, g_two]), "space", space_count)
    g_one = summed[0]
    g_two = summed[1]

    embedded = jnp.concatenate(
        [jnp.concatenate([g_one, -g_two], axis=1), jnp.concatenate([g_two, g_one], axis=1)], axis=0
    )
    inv_root = inverse_root(embedded)
    z_top = inv_root[:block_count, :block_count]
    z_low = inv_root[block_count:, :block_count]
    coeff = jnp.concatenate(
        [jnp.concatenate([z_top.T, -z_low.T], axis=1), jnp.concatenate([z_low.T, z_top.T], axis=1)],
        axis=0,
    )
    kept_count = lax.dynamic_slice_in_dim(n_keep, lax.axis_index("tm"), 1)
    kept_rows = jnp.arange(rows, dtype=jnp.int32) % block_count < kept_count
    coeff = jnp.where(kept_rows[:, None], coeff, jnp.zeros_like(coeff)) * (1.0 / LINK_SCALE)
    coeff_halves = jnp.stack([jnp.dot(coeff, p, precision=HIGH) for p in pick])
    mode_field = mode_call(coeff_halves, high, low, 1024).reshape(1, 2, block_count, points_here)
    energy = (jnp.trace(g_one) / block_count).reshape(1)
    return (mode_field, energy)


def solution(mesh):
    placed = (P("tm", "space"), P("space"), P(), P())
    return jax.shard_map(
        shards,
        mesh=mesh,
        in_specs=placed,
        out_specs=(P("tm", None, None, "space"), P("tm")),
        check_vma=False,
    )
```

```python
import jax
import jax.numpy as jnp
from jax import lax
from jax.sharding import PartitionSpec as P
from jax.experimental import pallas as pl
from jax.experimental.pallas import tpu as pltpu

NT = 64
NS_STEPS = 4
HIGH = lax.Precision.HIGHEST
LINK_SCALE = 128.0


def spectra_table(freqs):
    time_int = jnp.arange(NT, dtype=jnp.int32)
    time_float = time_int.astype(jnp.float32)
    window = 0.5 - 0.5 * jnp.cos(2.0 * jnp.pi * time_float / NT)
    norm = jnp.sqrt(jnp.sum(window * window))
    wrapped = freqs[:, None] * time_int[None, :] % NT
    phase_angle = 2.0 * jnp.pi * wrapped.astype(jnp.float32) / NT
    real_rows = window[None, :] * jnp.cos(phase_angle) / norm
    imag_rows = -window[None, :] * jnp.sin(phase_angle) / norm
    return jnp.concatenate([real_rows, imag_rows], axis=0).astype(jnp.bfloat16)


def transform_blocks(dft_table, snapshots, freq_count, halves):
    local_blocks = snapshots.shape[0] // NT
    points = snapshots.shape[1]
    table_view = dft_table.reshape(2, freq_count, NT).transpose(1, 0, 2)
    chooser = jnp.eye(local_blocks, dtype=dft_table.dtype)
    lifted = table_view[:, :, None, None, :] * chooser[None, None, :, :, None]
    lifted = lifted.reshape(freq_count * 2 * local_blocks, local_blocks * NT)
    split_view = snapshots.reshape(local_blocks * NT, halves, points // halves)
    spectra = jnp.einsum("qc,chp->qhp", lifted, split_view, preferred_element_type=jnp.float32)
    return spectra.reshape(freq_count * 2 * local_blocks * halves, points // halves)


def split_pair(value):
    rounded = lax.reduce_precision(value, exponent_bits=8, mantissa_bits=7)
    return rounded.astype(jnp.bfloat16), (value - rounded).astype(jnp.bfloat16)


NT_DIMS = (((1,), (1,)), ((), ()))


def gram_kernel(hi_ref, lo_ref, w_ref, o_ref):
    @pl.when(pl.program_id(0) == 0)
    def _():
        o_ref[...] = jnp.zeros_like(o_ref)

    x_hi = hi_ref[...]
    x_lo = lo_ref[...]
    x = x_hi.astype(jnp.float32) + x_lo.astype(jnp.float32)
    odd = lax.broadcasted_iota(jnp.int32, x.shape, 0) % 2 == 1
    row_weights = jnp.where(odd, w_ref[1:2, :], w_ref[0:1, :])
    y_hi, y_lo = split_pair(x * row_weights)
    acc = lax.dot_general(x_hi, y_hi, NT_DIMS, preferred_element_type=jnp.float32)
    acc += lax.dot_general(x_lo, y_hi, NT_DIMS, preferred_element_type=jnp.float32)
    acc += lax.dot_general(x_hi, y_lo, NT_DIMS, preferred_element_type=jnp.float32)
    o_ref[...] += acc


def gram_call(high, low, weights, chunk):
    rows, points = high.shape
    return pl.pallas_call(
        gram_kernel,
        grid=(points // chunk,),
        in_specs=[
            pl.BlockSpec((rows, chunk), lambda k: (0, k)),
            pl.BlockSpec((rows, chunk), lambda k: (0, k)),
            pl.BlockSpec((2, chunk), lambda k: (0, k)),
        ],
        out_specs=pl.BlockSpec((rows, rows), lambda k: (0, 0)),
        out_shape=jax.ShapeDtypeStruct((rows, rows), jnp.float32),
        cost_estimate=pl.CostEstimate(
            flops=6 * rows * rows * points, transcendentals=0, bytes_accessed=4 * rows * points
        ),
    )(high, low, weights.reshape(2, points))


def mode_kernel(c_hi_ref, c_lo_ref, hi_ref, lo_ref, o_ref):
    x_hi = hi_ref[...]
    x_lo = lo_ref[...]
    c_hi = c_hi_ref[...]
    acc = jnp.dot(c_hi, x_hi, preferred_element_type=jnp.float32)
    acc += jnp.dot(c_lo_ref[...], x_hi, preferred_element_type=jnp.float32)
    acc += jnp.dot(c_hi, x_lo, preferred_element_type=jnp.float32)
    o_ref[...] = acc.astype(o_ref.dtype)


def mode_call(coeff_halves, high, low, chunk):
    halves, out_rows, rows = coeff_halves.shape
    points = high.shape[1]
    steps = points // chunk
    c_hi, c_lo = split_pair(coeff_halves)
    return pl.pallas_call(
        mode_kernel,
        grid=(halves, steps),
        in_specs=[
            pl.BlockSpec((None, out_rows, rows), lambda h, k: (h, 0, 0)),
            pl.BlockSpec((None, out_rows, rows), lambda h, k: (h, 0, 0)),
            pl.BlockSpec((rows, chunk), lambda h, k: (0, k)),
            pl.BlockSpec((rows, chunk), lambda h, k: (0, k)),
        ],
        out_specs=pl.BlockSpec((out_rows, chunk), lambda h, k: (0, h * steps + k)),
        out_shape=jax.ShapeDtypeStruct((out_rows, halves * points), jnp.bfloat16),
        cost_estimate=pl.CostEstimate(
            flops=6 * out_rows * rows * points * halves,
            transcendentals=0,
            bytes_accessed=4 * rows * points * halves + 2 * out_rows * points * halves,
        ),
    )(c_hi, c_lo, high, low)


def butterfly_sum(value, axis, size):
    step = 1
    while step < size:
        pairs = [(i, i ^ step) for i in range(size)]
        value = value + lax.ppermute(value, axis, pairs)
        step *= 2
    return value


def inverse_root(embedded):
    size_two = embedded.shape[0]
    frobenius = jnp.sqrt(jnp.sum(embedded * embedded) + 1e-06)
    identity = jnp.eye(size_two, dtype=jnp.float32)
    current = embedded / frobenius
    result = identity
    for sweep in range(NS_STEPS):
        factor = 1.5 * identity - 0.5 * jnp.dot(result, current, precision=HIGH)
        current = jnp.dot(current, factor, precision=HIGH)
        result = jnp.dot(factor, result, precision=HIGH)
    return result


def shards(data, weights, freqs, n_keep):
    tm_count = lax.axis_size("tm")
    space_count = lax.axis_size("space")
    freq_count = freqs.shape[0]
    points_here = data.shape[1]
    total_points = points_here * space_count
    local_blocks = data.shape[0] // NT
    block_count = local_blocks * tm_count
    rows = 2 * block_count

    dft_table = spectra_table(freqs)
    halves = 2
    spectra = transform_blocks(dft_table, data, freq_count, halves)
    sent = (spectra * LINK_SCALE).astype(jnp.float16)
    received = lax.all_to_all(sent, "tm", split_axis=0, concat_axis=0, tiled=True)
    high, low = split_pair(received.astype(jnp.float32))
    recv_rows = received.shape[0]

    square = gram_call(high, low, weights, 1024) * (1.0 / (LINK_SCALE * LINK_SCALE * total_points))
    natural = jnp.arange(rows, dtype=jnp.int32)
    part, block = natural // block_count, natural % block_count
    home = (block // local_blocks) * (2 * local_blocks * halves) + part * (local_blocks * halves) + (block % local_blocks) * halves
    recv_index = jnp.arange(recv_rows, dtype=jnp.int32)
    pick = [(recv_index[None, :] == (home + h)[:, None]).astype(jnp.float32) for h in range(halves)]
    same_half = recv_index[:, None] % halves == recv_index[None, :] % halves
    either = pick[0] + pick[1]
    square = jnp.where(same_half, square, jnp.zeros_like(square))
    square = jnp.dot(jnp.dot(either, square, precision=HIGH), either.T, precision=HIGH)
    g_one = square[:block_count, :block_count] + square[block_count:, block_count:]
    g_two = square[:block_count, block_count:] - square[block_count:, :block_count]
    lower = jnp.arange(block_count)[:, None] > jnp.arange(block_count)[None, :]
    packed = jnp.where(lower, g_two, g_one)
    spread = jnp.broadcast_to(packed[None], (space_count, block_count, block_count))
    partials = lax.all_to_all(spread, "space", split_axis=0, concat_axis=0, tiled=True)
    total = jnp.sum(partials, axis=0)
    upper = jnp.where(lower, jnp.zeros_like(total), total)
    strict = jnp.where(lower, total, jnp.zeros_like(total))
    g_one = upper + jnp.where(lower, upper.T, jnp.zeros_like(total))
    g_two = strict - strict.T

    embedded = jnp.concatenate(
        [jnp.concatenate([g_one, -g_two], axis=1), jnp.concatenate([g_two, g_one], axis=1)], axis=0
    )
    inv_root = inverse_root(embedded)
    z_top = inv_root[:block_count, :block_count]
    z_low = inv_root[block_count:, :block_count]
    coeff = jnp.concatenate(
        [jnp.concatenate([z_top.T, -z_low.T], axis=1), jnp.concatenate([z_low.T, z_top.T], axis=1)],
        axis=0,
    )
    kept_count = lax.dynamic_slice_in_dim(n_keep, lax.axis_index("tm"), 1)
    kept_rows = jnp.arange(rows, dtype=jnp.int32) % block_count < kept_count
    coeff = jnp.where(kept_rows[:, None], coeff, jnp.zeros_like(coeff)) * (1.0 / LINK_SCALE)
    coeff_halves = jnp.stack([jnp.dot(coeff, p, precision=HIGH) for p in pick])
    mode_field = mode_call(coeff_halves, high, low, 1024).reshape(1, 2, block_count, points_here)
    energy = (jnp.trace(g_one) / block_count).reshape(1)
    return (mode_field, energy)


def solution(mesh):
    placed = (P("tm", "space"), P("space"), P(), P())
    return jax.shard_map(
        shards,
        mesh=mesh,
        in_specs=placed,
        out_specs=(P("tm", None, None, "space"), P("tm")),
        check_vma=False,
    )
```

```python
import functools

import jax
import jax.numpy as jnp
from jax import lax
from jax.sharding import PartitionSpec as P
from jax.experimental import pallas as pl
from jax.experimental.pallas import tpu as pltpu

NT = 64
NS_STEPS = 4
HIGH = lax.Precision.HIGHEST
LINK_SCALE = 128.0


def spectra_table(freqs):
    time_int = jnp.arange(NT, dtype=jnp.int32)
    time_float = time_int.astype(jnp.float32)
    window = 0.5 - 0.5 * jnp.cos(2.0 * jnp.pi * time_float / NT)
    norm = jnp.sqrt(jnp.sum(window * window))
    wrapped = freqs[:, None] * time_int[None, :] % NT
    phase_angle = 2.0 * jnp.pi * wrapped.astype(jnp.float32) / NT
    real_rows = window[None, :] * jnp.cos(phase_angle) / norm
    imag_rows = -window[None, :] * jnp.sin(phase_angle) / norm
    return jnp.concatenate([real_rows, imag_rows], axis=0).astype(jnp.bfloat16)


def transform_blocks(dft_table, snapshots, freq_count, halves):
    local_blocks = snapshots.shape[0] // NT
    points = snapshots.shape[1] // halves
    table_view = dft_table.reshape(2, freq_count, NT).transpose(1, 0, 2)
    chooser = jnp.eye(local_blocks, dtype=dft_table.dtype)
    halver = jnp.eye(halves, dtype=dft_table.dtype)
    lifted = (
        table_view[:, None, :, None, None, None, :]
        * halver[None, :, None, None, :, None, None]
        * chooser[None, None, None, :, None, :, None]
    )
    lifted = lifted.reshape(freq_count * halves * 2 * local_blocks, halves * local_blocks * NT)
    stacked = jnp.concatenate([snapshots[:, h * points:(h + 1) * points] for h in range(halves)], axis=0)
    return jnp.dot(lifted, stacked, preferred_element_type=jnp.float32)


def split_pair(value):
    rounded = lax.reduce_precision(value, exponent_bits=8, mantissa_bits=7)
    return rounded.astype(jnp.bfloat16), (value - rounded).astype(jnp.bfloat16)


NT_DIMS = (((1,), (1,)), ((), ()))


def gram_kernel(group, hi_ref, lo_ref, w_ref, o_ref):
    @pl.when(pl.program_id(0) == 0)
    def _():
        o_ref[...] = jnp.zeros_like(o_ref)

    x_hi = hi_ref[...]
    x_lo = lo_ref[...]
    x = x_hi.astype(jnp.float32) + x_lo.astype(jnp.float32)
    odd = lax.broadcasted_iota(jnp.int32, x.shape, 0) // group % 2 == 1
    row_weights = jnp.where(odd, w_ref[1:2, :], w_ref[0:1, :])
    y_hi, y_lo = split_pair(x * row_weights)
    acc = lax.dot_general(x_hi, y_hi, NT_DIMS, preferred_element_type=jnp.float32)
    acc += lax.dot_general(x_lo, y_hi, NT_DIMS, preferred_element_type=jnp.float32)
    acc += lax.dot_general(x_hi, y_lo, NT_DIMS, preferred_element_type=jnp.float32)
    o_ref[...] += acc


def gram_call(high, low, weights, chunk, group):
    rows, points = high.shape
    return pl.pallas_call(
        functools.partial(gram_kernel, group),
        grid=(points // chunk,),
        in_specs=[
            pl.BlockSpec((rows, chunk), lambda k: (0, k)),
            pl.BlockSpec((rows, chunk), lambda k: (0, k)),
            pl.BlockSpec((2, chunk), lambda k: (0, k)),
        ],
        out_specs=pl.BlockSpec((rows, rows), lambda k: (0, 0)),
        out_shape=jax.ShapeDtypeStruct((rows, rows), jnp.float32),
        cost_estimate=pl.CostEstimate(
            flops=6 * rows * rows * points, transcendentals=0, bytes_accessed=4 * rows * points
        ),
    )(high, low, weights.reshape(2, points))


def mode_kernel(c_hi_ref, c_lo_ref, hi_ref, lo_ref, o_ref):
    x_hi = hi_ref[...]
    x_lo = lo_ref[...]
    c_hi = c_hi_ref[...]
    acc = jnp.dot(c_hi, x_hi, preferred_element_type=jnp.float32)
    acc += jnp.dot(c_lo_ref[...], x_hi, preferred_element_type=jnp.float32)
    acc += jnp.dot(c_hi, x_lo, preferred_element_type=jnp.float32)
    o_ref[...] = acc.astype(o_ref.dtype)


def mode_call(coeff_halves, high, low, chunk):
    halves, out_rows, rows = coeff_halves.shape
    points = high.shape[1]
    steps = points // chunk
    c_hi, c_lo = split_pair(coeff_halves)
    return pl.pallas_call(
        mode_kernel,
        grid=(halves, steps),
        in_specs=[
            pl.BlockSpec((None, out_rows, rows), lambda h, k: (h, 0, 0)),
            pl.BlockSpec((None, out_rows, rows), lambda h, k: (h, 0, 0)),
            pl.BlockSpec((rows, chunk), lambda h, k: (0, k)),
            pl.BlockSpec((rows, chunk), lambda h, k: (0, k)),
        ],
        out_specs=pl.BlockSpec((out_rows, chunk), lambda h, k: (0, h * steps + k)),
        out_shape=jax.ShapeDtypeStruct((out_rows, halves * points), jnp.bfloat16),
        cost_estimate=pl.CostEstimate(
            flops=6 * out_rows * rows * points * halves,
            transcendentals=0,
            bytes_accessed=4 * rows * points * halves + 2 * out_rows * points * halves,
        ),
    )(c_hi, c_lo, high, low)


def butterfly_sum(value, axis, size):
    step = 1
    while step < size:
        pairs = [(i, i ^ step) for i in range(size)]
        value = value + lax.ppermute(value, axis, pairs)
        step *= 2
    return value


def inverse_root(embedded):
    size_two = embedded.shape[0]
    frobenius = jnp.sqrt(jnp.sum(embedded * embedded) + 1e-06)
    identity = jnp.eye(size_two, dtype=jnp.float32)
    current = embedded / frobenius
    result = identity
    for sweep in range(NS_STEPS):
        factor = 1.5 * identity - 0.5 * jnp.dot(result, current, precision=HIGH)
        current = jnp.dot(current, factor, precision=HIGH)
        result = jnp.dot(factor, result, precision=HIGH)
    return result


def shards(data, weights, freqs, n_keep):
    tm_count = lax.axis_size("tm")
    space_count = lax.axis_size("space")
    freq_count = freqs.shape[0]
    points_here = data.shape[1]
    total_points = points_here * space_count
    local_blocks = data.shape[0] // NT
    block_count = local_blocks * tm_count
    rows = 2 * block_count

    dft_table = spectra_table(freqs)
    halves = 2
    spectra = transform_blocks(dft_table, data, freq_count, halves)
    sent = (spectra * LINK_SCALE).astype(jnp.float16)
    received = lax.all_to_all(sent, "tm", split_axis=0, concat_axis=0, tiled=True)
    high, low = split_pair(received.astype(jnp.float32))
    recv_rows = received.shape[0]

    square = gram_call(high, low, weights, 1024, 2 * local_blocks) * (1.0 / (LINK_SCALE * LINK_SCALE * total_points))
    natural = jnp.arange(rows, dtype=jnp.int32)
    part, block = natural // block_count, natural % block_count
    group = 2 * local_blocks
    home = (block // local_blocks) * (group * halves) + part * local_blocks + block % local_blocks
    recv_index = jnp.arange(recv_rows, dtype=jnp.int32)
    pick = [(recv_index[None, :] == (home + h * group)[:, None]).astype(jnp.float32) for h in range(halves)]
    row_half = recv_index // group % halves
    same_half = row_half[:, None] == row_half[None, :]
    either = pick[0] + pick[1]
    square = jnp.where(same_half, square, jnp.zeros_like(square))
    square = jnp.dot(jnp.dot(either, square, precision=HIGH), either.T, precision=HIGH)
    g_one = square[:block_count, :block_count] + square[block_count:, block_count:]
    g_two = square[:block_count, block_count:] - square[block_count:, :block_count]
    lower = jnp.arange(block_count)[:, None] > jnp.arange(block_count)[None, :]
    packed = jnp.where(lower, g_two, g_one)
    spread = jnp.broadcast_to(packed[None], (space_count, block_count, block_count))
    partials = lax.all_to_all(spread, "space", split_axis=0, concat_axis=0, tiled=True)
    total = jnp.sum(partials, axis=0)
    upper = jnp.where(lower, jnp.zeros_like(total), total)
    strict = jnp.where(lower, total, jnp.zeros_like(total))
    g_one = upper + jnp.where(lower, upper.T, jnp.zeros_like(total))
    g_two = strict - strict.T

    embedded = jnp.concatenate(
        [jnp.concatenate([g_one, -g_two], axis=1), jnp.concatenate([g_two, g_one], axis=1)], axis=0
    )
    inv_root = inverse_root(embedded)
    z_top = inv_root[:block_count, :block_count]
    z_low = inv_root[block_count:, :block_count]
    coeff = jnp.concatenate(
        [jnp.concatenate([z_top.T, -z_low.T], axis=1), jnp.concatenate([z_low.T, z_top.T], axis=1)],
        axis=0,
    )
    kept_count = lax.dynamic_slice_in_dim(n_keep, lax.axis_index("tm"), 1)
    kept_rows = jnp.arange(rows, dtype=jnp.int32) % block_count < kept_count
    coeff = jnp.where(kept_rows[:, None], coeff, jnp.zeros_like(coeff)) * (1.0 / LINK_SCALE)
    coeff_halves = jnp.stack([jnp.dot(coeff, p, precision=HIGH) for p in pick])
    mode_field = mode_call(coeff_halves, high, low, 2048).reshape(1, 2, block_count, points_here)
    energy = (jnp.trace(g_one) / block_count).reshape(1)
    return (mode_field, energy)


def solution(mesh):
    placed = (P("tm", "space"), P("space"), P(), P())
    return jax.shard_map(
        shards,
        mesh=mesh,
        in_specs=placed,
        out_specs=(P("tm", None, None, "space"), P("tm")),
        check_vma=False,
    )
```

```python
import functools

import jax
import jax.numpy as jnp
from jax import lax
from jax.sharding import PartitionSpec as P
from jax.experimental import pallas as pl
from jax.experimental.pallas import tpu as pltpu

NT = 64
NS_STEPS = 4
HIGH = lax.Precision.HIGHEST
LINK_SCALE = 128.0


def spectra_table(freqs):
    time_int = jnp.arange(NT, dtype=jnp.int32)
    time_float = time_int.astype(jnp.float32)
    window = 0.5 - 0.5 * jnp.cos(2.0 * jnp.pi * time_float / NT)
    norm = jnp.sqrt(jnp.sum(window * window))
    wrapped = freqs[:, None] * time_int[None, :] % NT
    phase_angle = 2.0 * jnp.pi * wrapped.astype(jnp.float32) / NT
    real_rows = window[None, :] * jnp.cos(phase_angle) / norm
    imag_rows = -window[None, :] * jnp.sin(phase_angle) / norm
    return jnp.concatenate([real_rows, imag_rows], axis=0).astype(jnp.bfloat16)


def transform_blocks(dft_table, snapshots, freq_count, halves):
    local_blocks = snapshots.shape[0] // NT
    points = snapshots.shape[1] // halves
    table_view = dft_table.reshape(2, freq_count, NT).transpose(1, 0, 2)
    chooser = jnp.eye(local_blocks, dtype=dft_table.dtype)
    halver = jnp.eye(halves, dtype=dft_table.dtype)
    lifted = (
        table_view[:, None, :, None, None, None, :]
        * halver[None, :, None, None, :, None, None]
        * chooser[None, None, None, :, None, :, None]
    )
    lifted = lifted.reshape(freq_count * halves * 2 * local_blocks, halves * local_blocks * NT)
    stacked = jnp.concatenate([snapshots[:, h * points:(h + 1) * points] for h in range(halves)], axis=0)
    return jnp.dot(lifted, stacked, preferred_element_type=jnp.float32)


def split_pair(value):
    rounded = lax.reduce_precision(value, exponent_bits=8, mantissa_bits=7)
    return rounded.astype(jnp.bfloat16), (value - rounded).astype(jnp.bfloat16)


NT_DIMS = (((1,), (1,)), ((), ()))


def gram_kernel(group, hi_ref, lo_ref, w_ref, o_ref):
    @pl.when(pl.program_id(0) == 0)
    def _():
        o_ref[...] = jnp.zeros_like(o_ref)

    x_hi = hi_ref[...]
    x_lo = lo_ref[...]
    x = x_hi.astype(jnp.float32) + x_lo.astype(jnp.float32)
    odd = lax.broadcasted_iota(jnp.int32, x.shape, 0) // group % 2 == 1
    row_weights = jnp.where(odd, w_ref[1:2, :], w_ref[0:1, :])
    y_hi, y_lo = split_pair(x * row_weights)
    acc = lax.dot_general(x_hi, y_hi, NT_DIMS, preferred_element_type=jnp.float32)
    acc += lax.dot_general(x_lo, y_hi, NT_DIMS, preferred_element_type=jnp.float32)
    acc += lax.dot_general(x_hi, y_lo, NT_DIMS, preferred_element_type=jnp.float32)
    o_ref[...] += acc


def gram_call(high, low, weights, chunk, group):
    rows, points = high.shape
    return pl.pallas_call(
        functools.partial(gram_kernel, group),
        grid=(points // chunk,),
        in_specs=[
            pl.BlockSpec((rows, chunk), lambda k: (0, k)),
            pl.BlockSpec((rows, chunk), lambda k: (0, k)),
            pl.BlockSpec((2, chunk), lambda k: (0, k)),
        ],
        out_specs=pl.BlockSpec((rows, rows), lambda k: (0, 0)),
        out_shape=jax.ShapeDtypeStruct((rows, rows), jnp.float32),
        cost_estimate=pl.CostEstimate(
            flops=6 * rows * rows * points, transcendentals=0, bytes_accessed=4 * rows * points
        ),
    )(high, low, weights.reshape(2, points))


def mode_kernel(c_hi_ref, c_lo_ref, hi_ref, lo_ref, o_ref):
    x_hi = hi_ref[...]
    x_lo = lo_ref[...]
    c_hi = c_hi_ref[...]
    acc = jnp.dot(c_hi, x_hi, preferred_element_type=jnp.float32)
    acc += jnp.dot(c_lo_ref[...], x_hi, preferred_element_type=jnp.float32)
    acc += jnp.dot(c_hi, x_lo, preferred_element_type=jnp.float32)
    o_ref[...] = acc.astype(o_ref.dtype)


def mode_call(coeff_halves, high, low, chunk):
    halves, out_rows, rows = coeff_halves.shape
    points = high.shape[1]
    steps = points // chunk
    c_hi, c_lo = split_pair(coeff_halves)
    return pl.pallas_call(
        mode_kernel,
        grid=(halves, steps),
        in_specs=[
            pl.BlockSpec((None, out_rows, rows), lambda h, k: (h, 0, 0)),
            pl.BlockSpec((None, out_rows, rows), lambda h, k: (h, 0, 0)),
            pl.BlockSpec((rows, chunk), lambda h, k: (0, k)),
            pl.BlockSpec((rows, chunk), lambda h, k: (0, k)),
        ],
        out_specs=pl.BlockSpec((out_rows, chunk), lambda h, k: (0, h * steps + k)),
        out_shape=jax.ShapeDtypeStruct((out_rows, halves * points), jnp.bfloat16),
        cost_estimate=pl.CostEstimate(
            flops=6 * out_rows * rows * points * halves,
            transcendentals=0,
            bytes_accessed=4 * rows * points * halves + 2 * out_rows * points * halves,
        ),
    )(c_hi, c_lo, high, low)


def butterfly_sum(value, axis, size):
    step = 1
    while step < size:
        pairs = [(i, i ^ step) for i in range(size)]
        value = value + lax.ppermute(value, axis, pairs)
        step *= 2
    return value


def inverse_root(embedded):
    size_two = embedded.shape[0]
    frobenius = jnp.sqrt(jnp.sum(embedded * embedded) + 1e-06)
    identity = jnp.eye(size_two, dtype=jnp.float32)
    current = embedded / frobenius
    result = identity
    for sweep in range(NS_STEPS):
        factor = 1.5 * identity - 0.5 * jnp.dot(result, current, precision=HIGH)
        current = jnp.dot(current, factor, precision=HIGH)
        result = jnp.dot(factor, result, precision=HIGH)
    return result


def shards(data, weights, freqs, n_keep):
    tm_count = lax.axis_size("tm")
    space_count = lax.axis_size("space")
    freq_count = freqs.shape[0]
    points_here = data.shape[1]
    total_points = points_here * space_count
    local_blocks = data.shape[0] // NT
    block_count = local_blocks * tm_count
    rows = 2 * block_count

    dft_table = spectra_table(freqs)
    halves = 2
    spectra = transform_blocks(dft_table, data, freq_count, halves)
    sent = (spectra * LINK_SCALE).astype(jnp.float16)
    received = lax.all_to_all(sent, "tm", split_axis=0, concat_axis=0, tiled=True)
    high, low = split_pair(received.astype(jnp.float32))
    recv_rows = received.shape[0]

    square = gram_call(high, low, weights, 2048, 2 * local_blocks) * (1.0 / (LINK_SCALE * LINK_SCALE * total_points))
    natural = jnp.arange(rows, dtype=jnp.int32)
    part, block = natural // block_count, natural % block_count
    group = 2 * local_blocks
    home = (block // local_blocks) * (group * halves) + part * local_blocks + block % local_blocks
    recv_index = jnp.arange(recv_rows, dtype=jnp.int32)
    pick = [(recv_index[None, :] == (home + h * group)[:, None]).astype(jnp.float32) for h in range(halves)]
    row_half = recv_index // group % halves
    same_half = row_half[:, None] == row_half[None, :]
    either = pick[0] + pick[1]
    square = jnp.where(same_half, square, jnp.zeros_like(square))
    square = jnp.dot(jnp.dot(either, square, precision=HIGH), either.T, precision=HIGH)
    g_one = square[:block_count, :block_count] + square[block_count:, block_count:]
    g_two = square[:block_count, block_count:] - square[block_count:, :block_count]
    packed = jnp.concatenate([g_one, g_two], axis=1)
    spread = jnp.broadcast_to(packed[None], (space_count,) + packed.shape)
    partials = lax.all_to_all(spread, "space", split_axis=0, concat_axis=0, tiled=True)
    total = jnp.sum(partials, axis=0)
    g_one = total[:, :block_count]
    g_two = total[:, block_count:]

    embedded = jnp.concatenate(
        [jnp.concatenate([g_one, -g_two], axis=1), jnp.concatenate([g_two, g_one], axis=1)], axis=0
    )
    inv_root = inverse_root(embedded)
    z_top = inv_root[:block_count, :block_count]
    z_low = inv_root[block_count:, :block_count]
    coeff = jnp.concatenate(
        [jnp.concatenate([z_top.T, -z_low.T], axis=1), jnp.concatenate([z_low.T, z_top.T], axis=1)],
        axis=0,
    )
    kept_count = lax.dynamic_slice_in_dim(n_keep, lax.axis_index("tm"), 1)
    kept_rows = jnp.arange(rows, dtype=jnp.int32) % block_count < kept_count
    coeff = jnp.where(kept_rows[:, None], coeff, jnp.zeros_like(coeff)) * (1.0 / LINK_SCALE)
    coeff_halves = jnp.stack([jnp.dot(coeff, p, precision=HIGH) for p in pick])
    mode_field = mode_call(coeff_halves, high, low, 2048).reshape(1, 2, block_count, points_here)
    energy = (jnp.trace(g_one) / block_count).reshape(1)
    return (mode_field, energy)


def solution(mesh):
    placed = (P("tm", "space"), P("space"), P(), P())
    return jax.shard_map(
        shards,
        mesh=mesh,
        in_specs=placed,
        out_specs=(P("tm", None, None, "space"), P("tm")),
        check_vma=False,
    )
```

```python
import functools

import jax
import jax.numpy as jnp
from jax import lax
from jax.sharding import PartitionSpec as P
from jax.experimental import pallas as pl
from jax.experimental.pallas import tpu as pltpu

NT = 64
NS_STEPS = 4
HIGH = lax.Precision.HIGHEST
LINK_SCALE = 128.0


def spectra_table(freqs):
    time_int = jnp.arange(NT, dtype=jnp.int32)
    time_float = time_int.astype(jnp.float32)
    window = 0.5 - 0.5 * jnp.cos(2.0 * jnp.pi * time_float / NT)
    norm = jnp.sqrt(jnp.sum(window * window))
    wrapped = freqs[:, None] * time_int[None, :] % NT
    phase_angle = 2.0 * jnp.pi * wrapped.astype(jnp.float32) / NT
    real_rows = window[None, :] * jnp.cos(phase_angle) / norm
    imag_rows = -window[None, :] * jnp.sin(phase_angle) / norm
    return jnp.concatenate([real_rows, imag_rows], axis=0).astype(jnp.bfloat16)


def transform_blocks(dft_table, snapshots, freq_count, halves):
    local_blocks = snapshots.shape[0] // NT
    points = snapshots.shape[1] // halves
    table_view = dft_table.reshape(2, freq_count, NT).transpose(1, 0, 2)
    chooser = jnp.eye(local_blocks, dtype=dft_table.dtype)
    halver = jnp.eye(halves, dtype=dft_table.dtype)
    lifted = (
        table_view[:, None, :, None, None, None, :]
        * halver[None, :, None, None, :, None, None]
        * chooser[None, None, None, :, None, :, None]
    )
    lifted = lifted.reshape(freq_count * halves * 2 * local_blocks, halves * local_blocks * NT)
    stacked = jnp.concatenate([snapshots[:, h * points:(h + 1) * points] for h in range(halves)], axis=0)
    return jnp.dot(lifted, stacked, preferred_element_type=jnp.float32)


def split_pair(value):
    rounded = lax.reduce_precision(value, exponent_bits=8, mantissa_bits=7)
    return rounded.astype(jnp.bfloat16), (value - rounded).astype(jnp.bfloat16)


NT_DIMS = (((1,), (1,)), ((), ()))


def gram_kernel(group, hi_ref, lo_ref, w_ref, o_ref):
    @pl.when(pl.program_id(0) == 0)
    def _():
        o_ref[...] = jnp.zeros_like(o_ref)

    x_hi = hi_ref[...]
    x_lo = lo_ref[...]
    x = x_hi.astype(jnp.float32) + x_lo.astype(jnp.float32)
    odd = lax.broadcasted_iota(jnp.int32, x.shape, 0) // group % 2 == 1
    row_weights = jnp.where(odd, w_ref[1:2, :], w_ref[0:1, :])
    y_hi, y_lo = split_pair(x * row_weights)
    acc = lax.dot_general(x_hi, y_hi, NT_DIMS, preferred_element_type=jnp.float32)
    acc += lax.dot_general(x_lo, y_hi, NT_DIMS, preferred_element_type=jnp.float32)
    acc += lax.dot_general(x_hi, y_lo, NT_DIMS, preferred_element_type=jnp.float32)
    o_ref[...] += acc


def gram_call(high, low, weights, chunk, group):
    rows, points = high.shape
    return pl.pallas_call(
        functools.partial(gram_kernel, group),
        grid=(points // chunk,),
        in_specs=[
            pl.BlockSpec((rows, chunk), lambda k: (0, k)),
            pl.BlockSpec((rows, chunk), lambda k: (0, k)),
            pl.BlockSpec((2, chunk), lambda k: (0, k)),
        ],
        out_specs=pl.BlockSpec((rows, rows), lambda k: (0, 0)),
        out_shape=jax.ShapeDtypeStruct((rows, rows), jnp.float32),
        cost_estimate=pl.CostEstimate(
            flops=6 * rows * rows * points, transcendentals=0, bytes_accessed=4 * rows * points
        ),
    )(high, low, weights.reshape(2, points))


def mode_kernel(c_hi_ref, c_lo_ref, hi_ref, lo_ref, o_ref):
    x_hi = hi_ref[...]
    x_lo = lo_ref[...]
    c_hi = c_hi_ref[...]
    acc = jnp.dot(c_hi, x_hi, preferred_element_type=jnp.float32)
    acc += jnp.dot(c_lo_ref[...], x_hi, preferred_element_type=jnp.float32)
    acc += jnp.dot(c_hi, x_lo, preferred_element_type=jnp.float32)
    o_ref[...] = acc.astype(o_ref.dtype)


def mode_call(coeff_halves, high, low, chunk):
    halves, out_rows, rows = coeff_halves.shape
    points = high.shape[1]
    steps = points // chunk
    c_hi, c_lo = split_pair(coeff_halves)
    return pl.pallas_call(
        mode_kernel,
        grid=(steps, halves),
        in_specs=[
            pl.BlockSpec((None, out_rows, rows), lambda k, h: (h, 0, 0)),
            pl.BlockSpec((None, out_rows, rows), lambda k, h: (h, 0, 0)),
            pl.BlockSpec((rows, chunk), lambda k, h: (0, k)),
            pl.BlockSpec((rows, chunk), lambda k, h: (0, k)),
        ],
        out_specs=pl.BlockSpec((out_rows, chunk), lambda k, h: (0, h * steps + k)),
        out_shape=jax.ShapeDtypeStruct((out_rows, halves * points), jnp.bfloat16),
        cost_estimate=pl.CostEstimate(
            flops=6 * out_rows * rows * points * halves,
            transcendentals=0,
            bytes_accessed=4 * rows * points * halves + 2 * out_rows * points * halves,
        ),
    )(c_hi, c_lo, high, low)


def butterfly_sum(value, axis, size):
    step = 1
    while step < size:
        pairs = [(i, i ^ step) for i in range(size)]
        value = value + lax.ppermute(value, axis, pairs)
        step *= 2
    return value


def inverse_root(embedded):
    size_two = embedded.shape[0]
    frobenius = jnp.sqrt(jnp.sum(embedded * embedded) + 1e-06)
    identity = jnp.eye(size_two, dtype=jnp.float32)
    current = embedded / frobenius
    factor = 1.5 * identity - 0.5 * current
    current = jnp.dot(current, factor, precision=HIGH)
    result = factor
    for sweep in range(1, NS_STEPS):
        factor = 1.5 * identity - 0.5 * jnp.dot(result, current, precision=HIGH)
        current = jnp.dot(current, factor, precision=HIGH)
        result = jnp.dot(factor, result, precision=HIGH)
    return result


def shards(data, weights, freqs, n_keep):
    tm_count = lax.axis_size("tm")
    space_count = lax.axis_size("space")
    freq_count = freqs.shape[0]
    points_here = data.shape[1]
    total_points = points_here * space_count
    local_blocks = data.shape[0] // NT
    block_count = local_blocks * tm_count
    rows = 2 * block_count

    dft_table = spectra_table(freqs)
    halves = 2
    spectra = transform_blocks(dft_table, data, freq_count, halves)
    sent = (spectra * LINK_SCALE).astype(jnp.float16)
    received = lax.all_to_all(sent, "tm", split_axis=0, concat_axis=0, tiled=True)
    high, low = split_pair(received.astype(jnp.float32))
    recv_rows = received.shape[0]

    square = gram_call(high, low, weights, 2048, 2 * local_blocks) * (1.0 / (LINK_SCALE * LINK_SCALE * total_points))
    natural = jnp.arange(rows, dtype=jnp.int32)
    part, block = natural // block_count, natural % block_count
    group = 2 * local_blocks
    home = (block // local_blocks) * (group * halves) + part * local_blocks + block % local_blocks
    recv_index = jnp.arange(recv_rows, dtype=jnp.int32)
    pick = [(recv_index[None, :] == (home + h * group)[:, None]).astype(jnp.float32) for h in range(halves)]
    row_half = recv_index // group % halves
    same_half = row_half[:, None] == row_half[None, :]
    either = pick[0] + pick[1]
    square = jnp.where(same_half, square, jnp.zeros_like(square))
    square = jnp.dot(jnp.dot(either, square, precision=HIGH), either.T, precision=HIGH)
    g_one = square[:block_count, :block_count] + square[block_count:, block_count:]
    g_two = square[:block_count, block_count:] - square[block_count:, :block_count]
    lower = jnp.arange(block_count)[:, None] > jnp.arange(block_count)[None, :]
    packed = jnp.where(lower, g_two, g_one)
    spread = jnp.broadcast_to(packed[None], (space_count, block_count, block_count))
    partials = lax.all_to_all(spread, "space", split_axis=0, concat_axis=0, tiled=True)
    total = jnp.sum(partials, axis=0)
    upper = jnp.where(lower, jnp.zeros_like(total), total)
    strict = jnp.where(lower, total, jnp.zeros_like(total))
    g_one = upper + jnp.where(lower, upper.T, jnp.zeros_like(total))
    g_two = strict - strict.T

    embedded = jnp.concatenate(
        [jnp.concatenate([g_one, -g_two], axis=1), jnp.concatenate([g_two, g_one], axis=1)], axis=0
    )
    inv_root = inverse_root(embedded)
    z_top = inv_root[:block_count, :block_count]
    z_low = inv_root[block_count:, :block_count]
    coeff = jnp.concatenate(
        [jnp.concatenate([z_top.T, -z_low.T], axis=1), jnp.concatenate([z_low.T, z_top.T], axis=1)],
        axis=0,
    )
    kept_count = lax.dynamic_slice_in_dim(n_keep, lax.axis_index("tm"), 1)
    kept_rows = jnp.arange(rows, dtype=jnp.int32) % block_count < kept_count
    coeff = jnp.where(kept_rows[:, None], coeff, jnp.zeros_like(coeff)) * (1.0 / LINK_SCALE)
    coeff_halves = jnp.stack([jnp.dot(coeff, p, precision=HIGH) for p in pick])
    mode_field = mode_call(coeff_halves, high, low, 2048).reshape(1, 2, block_count, points_here)
    energy = (jnp.trace(g_one) / block_count).reshape(1)
    return (mode_field, energy)


def solution(mesh):
    placed = (P("tm", "space"), P("space"), P(), P())
    return jax.shard_map(
        shards,
        mesh=mesh,
        in_specs=placed,
        out_specs=(P("tm", None, None, "space"), P("tm")),
        check_vma=False,
    )
```

```python
import functools

import jax
import jax.numpy as jnp
from jax import lax
from jax.sharding import PartitionSpec as P
from jax.experimental import pallas as pl
from jax.experimental.pallas import tpu as pltpu

NT = 64
NS_STEPS = 4
HIGH = lax.Precision.HIGHEST
LINK_SCALE = 128.0


def spectra_table(freqs):
    time_int = jnp.arange(NT, dtype=jnp.int32)
    time_float = time_int.astype(jnp.float32)
    window = 0.5 - 0.5 * jnp.cos(2.0 * jnp.pi * time_float / NT)
    norm = jnp.sqrt(jnp.sum(window * window))
    wrapped = freqs[:, None] * time_int[None, :] % NT
    phase_angle = 2.0 * jnp.pi * wrapped.astype(jnp.float32) / NT
    real_rows = window[None, :] * jnp.cos(phase_angle) / norm
    imag_rows = -window[None, :] * jnp.sin(phase_angle) / norm
    return jnp.concatenate([real_rows, imag_rows], axis=0).astype(jnp.bfloat16)


def transform_blocks(dft_table, snapshots, freq_count, halves):
    local_blocks = snapshots.shape[0] // NT
    points = snapshots.shape[1] // halves
    table_view = dft_table.reshape(2, freq_count, NT).transpose(1, 0, 2)
    chooser = jnp.eye(local_blocks, dtype=dft_table.dtype)
    halver = jnp.eye(halves, dtype=dft_table.dtype)
    lifted = (
        table_view[:, None, :, None, None, None, :]
        * halver[None, :, None, None, :, None, None]
        * chooser[None, None, None, :, None, :, None]
    )
    lifted = lifted.reshape(freq_count * halves * 2 * local_blocks, halves * local_blocks * NT)
    stacked = jnp.concatenate([snapshots[:, h * points:(h + 1) * points] for h in range(halves)], axis=0)
    return jnp.dot(lifted, stacked, preferred_element_type=jnp.float32)


def split_pair(value):
    rounded = lax.reduce_precision(value, exponent_bits=8, mantissa_bits=7)
    return rounded.astype(jnp.bfloat16), (value - rounded).astype(jnp.bfloat16)


NT_DIMS = (((1,), (1,)), ((), ()))


def gram_kernel(group, hi_ref, lo_ref, w_ref, o_ref):
    @pl.when(pl.program_id(0) == 0)
    def _():
        o_ref[...] = jnp.zeros_like(o_ref)

    x_hi = hi_ref[...]
    x_lo = lo_ref[...]
    x = x_hi.astype(jnp.float32) + x_lo.astype(jnp.float32)
    odd = lax.broadcasted_iota(jnp.int32, x.shape, 0) // group % 2 == 1
    row_weights = jnp.where(odd, w_ref[1:2, :], w_ref[0:1, :])
    y_hi, y_lo = split_pair(x * row_weights)
    acc = lax.dot_general(x_hi, y_hi, NT_DIMS, preferred_element_type=jnp.float32)
    acc += lax.dot_general(x_lo, y_hi, NT_DIMS, preferred_element_type=jnp.float32)
    acc += lax.dot_general(x_hi, y_lo, NT_DIMS, preferred_element_type=jnp.float32)
    o_ref[...] += acc


def gram_call(high, low, weights, chunk, group):
    rows, points = high.shape
    return pl.pallas_call(
        functools.partial(gram_kernel, group),
        grid=(points // chunk,),
        in_specs=[
            pl.BlockSpec((rows, chunk), lambda k: (0, k)),
            pl.BlockSpec((rows, chunk), lambda k: (0, k)),
            pl.BlockSpec((2, chunk), lambda k: (0, k)),
        ],
        out_specs=pl.BlockSpec((rows, rows), lambda k: (0, 0)),
        out_shape=jax.ShapeDtypeStruct((rows, rows), jnp.float32),
        cost_estimate=pl.CostEstimate(
            flops=6 * rows * rows * points, transcendentals=0, bytes_accessed=4 * rows * points
        ),
    )(high, low, weights.reshape(2, points))


def mode_kernel(c_hi_ref, c_lo_ref, hi_ref, lo_ref, o_ref):
    x_hi = hi_ref[...]
    x_lo = lo_ref[...]
    c_hi = c_hi_ref[...]
    acc = jnp.dot(c_hi, x_hi, preferred_element_type=jnp.float32)
    acc += jnp.dot(c_lo_ref[...], x_hi, preferred_element_type=jnp.float32)
    acc += jnp.dot(c_hi, x_lo, preferred_element_type=jnp.float32)
    o_ref[...] = acc.astype(o_ref.dtype)


def mode_call(coeff_halves, high, low, chunk):
    halves, out_rows, rows = coeff_halves.shape
    points = high.shape[1]
    steps = points // chunk
    c_hi, c_lo = split_pair(coeff_halves)
    return pl.pallas_call(
        mode_kernel,
        grid=(steps, halves),
        in_specs=[
            pl.BlockSpec((None, out_rows, rows), lambda k, h: (h, 0, 0)),
            pl.BlockSpec((None, out_rows, rows), lambda k, h: (h, 0, 0)),
            pl.BlockSpec((rows, chunk), lambda k, h: (0, k)),
            pl.BlockSpec((rows, chunk), lambda k, h: (0, k)),
        ],
        out_specs=pl.BlockSpec((out_rows, chunk), lambda k, h: (0, h * steps + k)),
        out_shape=jax.ShapeDtypeStruct((out_rows, halves * points), jnp.bfloat16),
        cost_estimate=pl.CostEstimate(
            flops=6 * out_rows * rows * points * halves,
            transcendentals=0,
            bytes_accessed=4 * rows * points * halves + 2 * out_rows * points * halves,
        ),
    )(c_hi, c_lo, high, low)


def butterfly_sum(value, axis, size):
    step = 1
    while step < size:
        pairs = [(i, i ^ step) for i in range(size)]
        value = value + lax.ppermute(value, axis, pairs)
        step *= 2
    return value


def inverse_root(embedded):
    size_two = embedded.shape[0]
    frobenius = jnp.sqrt(jnp.sum(embedded * embedded) + 1e-06)
    identity = jnp.eye(size_two, dtype=jnp.float32)
    current = embedded / frobenius
    factor = 1.5 * identity - 0.5 * current
    current = jnp.dot(current, factor, precision=HIGH)
    result = factor
    for sweep in range(1, NS_STEPS):
        factor = 1.5 * identity - 0.5 * jnp.dot(result, current, precision=HIGH)
        current = jnp.dot(current, factor, precision=HIGH)
        result = jnp.dot(factor, result, precision=HIGH)
    return result


def shards(data, weights, freqs, n_keep):
    tm_count = lax.axis_size("tm")
    space_count = lax.axis_size("space")
    freq_count = freqs.shape[0]
    points_here = data.shape[1]
    total_points = points_here * space_count
    local_blocks = data.shape[0] // NT
    block_count = local_blocks * tm_count
    rows = 2 * block_count

    dft_table = spectra_table(freqs)
    halves = 2
    spectra = transform_blocks(dft_table, data, freq_count, halves)
    sent = (spectra * LINK_SCALE).astype(jnp.float16)
    received = lax.all_to_all(sent, "tm", split_axis=0, concat_axis=0, tiled=True)
    high, low = split_pair(received.astype(jnp.float32))
    recv_rows = received.shape[0]

    square = gram_call(high, low, weights, 2048, 2 * local_blocks) * (1.0 / (LINK_SCALE * LINK_SCALE * total_points))
    natural = jnp.arange(rows, dtype=jnp.int32)
    part, block = natural // block_count, natural % block_count
    group = 2 * local_blocks
    home = (block // local_blocks) * (group * halves) + part * local_blocks + block % local_blocks
    recv_index = jnp.arange(recv_rows, dtype=jnp.int32)
    pick = [(recv_index[None, :] == (home + h * group)[:, None]).astype(jnp.float32) for h in range(halves)]
    row_half = recv_index // group % halves
    same_half = row_half[:, None] == row_half[None, :]
    either = pick[0] + pick[1]
    square = jnp.where(same_half, square, jnp.zeros_like(square))
    square = jnp.dot(jnp.dot(either, square, precision=HIGH), either.T, precision=HIGH)
    g_one = square[:block_count, :block_count] + square[block_count:, block_count:]
    g_two = square[:block_count, block_count:] - square[block_count:, :block_count]
    lower = jnp.arange(block_count)[:, None] > jnp.arange(block_count)[None, :]
    packed = jnp.where(lower, g_two, g_one)
    rows_half = block_count // 2
    packed = jnp.concatenate([packed[:rows_half], packed[rows_half:]], axis=1)
    spread = jnp.broadcast_to(packed[None], (space_count,) + packed.shape)
    partials = lax.all_to_all(spread, "space", split_axis=0, concat_axis=0, tiled=True)
    total = partials[0]
    for source in range(1, space_count):
        total = total + partials[source]
    total = jnp.concatenate([total[:, :block_count], total[:, block_count:]], axis=0)
    upper = jnp.where(lower, jnp.zeros_like(total), total)
    strict = jnp.where(lower, total, jnp.zeros_like(total))
    g_one = upper + jnp.where(lower, upper.T, jnp.zeros_like(total))
    g_two = strict - strict.T

    embedded = jnp.concatenate(
        [jnp.concatenate([g_one, -g_two], axis=1), jnp.concatenate([g_two, g_one], axis=1)], axis=0
    )
    inv_root = inverse_root(embedded)
    z_top = inv_root[:block_count, :block_count]
    z_low = inv_root[block_count:, :block_count]
    coeff = jnp.concatenate(
        [jnp.concatenate([z_top.T, -z_low.T], axis=1), jnp.concatenate([z_low.T, z_top.T], axis=1)],
        axis=0,
    )
    kept_count = lax.dynamic_slice_in_dim(n_keep, lax.axis_index("tm"), 1)
    kept_rows = jnp.arange(rows, dtype=jnp.int32) % block_count < kept_count
    coeff = jnp.where(kept_rows[:, None], coeff, jnp.zeros_like(coeff)) * (1.0 / LINK_SCALE)
    coeff_halves = jnp.stack([jnp.dot(coeff, p, precision=HIGH) for p in pick])
    mode_field = mode_call(coeff_halves, high, low, 2048).reshape(1, 2, block_count, points_here)
    energy = (jnp.trace(g_one) / block_count).reshape(1)
    return (mode_field, energy)


def solution(mesh):
    placed = (P("tm", "space"), P("space"), P(), P())
    return jax.shard_map(
        shards,
        mesh=mesh,
        in_specs=placed,
        out_specs=(P("tm", None, None, "space"), P("tm")),
        check_vma=False,
    )
```

```python
import functools

import jax
import jax.numpy as jnp
from jax import lax
from jax.sharding import PartitionSpec as P
from jax.experimental import pallas as pl
from jax.experimental.pallas import tpu as pltpu

NT = 64
NS_STEPS = 4
HIGH = lax.Precision.HIGHEST
LINK_SCALE = 128.0


def spectra_table(freqs):
    time_int = jnp.arange(NT, dtype=jnp.int32)
    time_float = time_int.astype(jnp.float32)
    window = 0.5 - 0.5 * jnp.cos(2.0 * jnp.pi * time_float / NT)
    norm = jnp.sqrt(jnp.sum(window * window))
    wrapped = freqs[:, None] * time_int[None, :] % NT
    phase_angle = 2.0 * jnp.pi * wrapped.astype(jnp.float32) / NT
    real_rows = window[None, :] * jnp.cos(phase_angle) / norm
    imag_rows = -window[None, :] * jnp.sin(phase_angle) / norm
    return jnp.concatenate([real_rows, imag_rows], axis=0).astype(jnp.bfloat16)


def transform_blocks(dft_table, snapshots, freq_count, halves, chunks):
    local_blocks = snapshots.shape[0] // NT
    points = snapshots.shape[1] // halves
    width = points // chunks
    table_view = dft_table.reshape(2, freq_count, NT).transpose(1, 0, 2)
    chooser = jnp.eye(local_blocks, dtype=dft_table.dtype)
    halver = jnp.eye(halves, dtype=dft_table.dtype)
    lifted = (
        table_view[:, None, :, None, None, None, :]
        * halver[None, :, None, None, :, None, None]
        * chooser[None, None, None, :, None, :, None]
    )
    lifted = lifted.reshape(freq_count * halves * 2 * local_blocks, halves * local_blocks * NT)
    out = []
    for c in range(chunks):
        stacked = jnp.concatenate(
            [snapshots[:, h * points + c * width:h * points + (c + 1) * width] for h in range(halves)], axis=0
        )
        out.append(jnp.dot(lifted, stacked, preferred_element_type=jnp.float32))
    return out


def split_pair(value):
    rounded = lax.reduce_precision(value, exponent_bits=8, mantissa_bits=7)
    return rounded.astype(jnp.bfloat16), (value - rounded).astype(jnp.bfloat16)


NT_DIMS = (((1,), (1,)), ((), ()))


def gram_kernel(group, hi_ref, lo_ref, w_ref, o_ref):
    @pl.when(pl.program_id(0) == 0)
    def _():
        o_ref[...] = jnp.zeros_like(o_ref)

    x_hi = hi_ref[...]
    x_lo = lo_ref[...]
    x = x_hi.astype(jnp.float32) + x_lo.astype(jnp.float32)
    odd = lax.broadcasted_iota(jnp.int32, x.shape, 0) // group % 2 == 1
    row_weights = jnp.where(odd, w_ref[1:2, :], w_ref[0:1, :])
    y_hi, y_lo = split_pair(x * row_weights)
    acc = lax.dot_general(x_hi, y_hi, NT_DIMS, preferred_element_type=jnp.float32)
    acc += lax.dot_general(x_lo, y_hi, NT_DIMS, preferred_element_type=jnp.float32)
    acc += lax.dot_general(x_hi, y_lo, NT_DIMS, preferred_element_type=jnp.float32)
    o_ref[...] += acc


def gram_call(high, low, weights, chunk, group):
    rows, points = high.shape
    return pl.pallas_call(
        functools.partial(gram_kernel, group),
        grid=(points // chunk,),
        in_specs=[
            pl.BlockSpec((rows, chunk), lambda k: (0, k)),
            pl.BlockSpec((rows, chunk), lambda k: (0, k)),
            pl.BlockSpec((2, chunk), lambda k: (0, k)),
        ],
        out_specs=pl.BlockSpec((rows, rows), lambda k: (0, 0)),
        out_shape=jax.ShapeDtypeStruct((rows, rows), jnp.float32),
        cost_estimate=pl.CostEstimate(
            flops=6 * rows * rows * points, transcendentals=0, bytes_accessed=4 * rows * points
        ),
    )(high, low, weights.reshape(2, points))


def mode_kernel(c_hi_ref, c_lo_ref, *refs):
    o_ref = refs[-1]
    pairs = refs[:-1]
    c = pl.program_id(0)
    c_hi = c_hi_ref[...]
    c_lo = c_lo_ref[...]
    for index in range(len(pairs) // 2):

        @pl.when(c == index)
        def _():
            x_hi = pairs[2 * index][...]
            x_lo = pairs[2 * index + 1][...]
            acc = jnp.dot(c_hi, x_hi, preferred_element_type=jnp.float32)
            acc += jnp.dot(c_lo, x_hi, preferred_element_type=jnp.float32)
            acc += jnp.dot(c_hi, x_lo, preferred_element_type=jnp.float32)
            o_ref[...] = acc.astype(o_ref.dtype)


def mode_call(coeff_halves, pieces):
    halves, out_rows, rows = coeff_halves.shape
    chunks = len(pieces)
    width = pieces[0][0].shape[1]
    c_hi, c_lo = split_pair(coeff_halves)
    whole = pl.BlockSpec((rows, width), lambda c, h: (0, 0))
    flat = [array for pair in pieces for array in pair]
    return pl.pallas_call(
        mode_kernel,
        grid=(chunks, halves),
        in_specs=[
            pl.BlockSpec((None, out_rows, rows), lambda c, h: (h, 0, 0)),
            pl.BlockSpec((None, out_rows, rows), lambda c, h: (h, 0, 0)),
        ]
        + [whole] * len(flat),
        out_specs=pl.BlockSpec((out_rows, width), lambda c, h: (0, h * chunks + c)),
        out_shape=jax.ShapeDtypeStruct((out_rows, halves * chunks * width), jnp.bfloat16),
        cost_estimate=pl.CostEstimate(
            flops=6 * out_rows * rows * width * chunks * halves,
            transcendentals=0,
            bytes_accessed=4 * rows * width * chunks + 2 * out_rows * width * chunks * halves,
        ),
    )(c_hi, c_lo, *flat)


def butterfly_sum(value, axis, size):
    step = 1
    while step < size:
        pairs = [(i, i ^ step) for i in range(size)]
        value = value + lax.ppermute(value, axis, pairs)
        step *= 2
    return value


def inverse_root(embedded):
    size_two = embedded.shape[0]
    frobenius = jnp.sqrt(jnp.sum(embedded * embedded) + 1e-06)
    identity = jnp.eye(size_two, dtype=jnp.float32)
    current = embedded / frobenius
    factor = 1.5 * identity - 0.5 * current
    current = jnp.dot(current, factor, precision=HIGH)
    result = factor
    for sweep in range(1, NS_STEPS):
        factor = 1.5 * identity - 0.5 * jnp.dot(result, current, precision=HIGH)
        current = jnp.dot(current, factor, precision=HIGH)
        result = jnp.dot(factor, result, precision=HIGH)
    return result


def shards(data, weights, freqs, n_keep):
    tm_count = lax.axis_size("tm")
    space_count = lax.axis_size("space")
    freq_count = freqs.shape[0]
    points_here = data.shape[1]
    total_points = points_here * space_count
    local_blocks = data.shape[0] // NT
    block_count = local_blocks * tm_count
    rows = 2 * block_count

    dft_table = spectra_table(freqs)
    halves = 2
    half_points = points_here // halves
    chunks = 2
    width = half_points // chunks
    pieces = []
    square = None
    split_weights = weights.reshape(halves, half_points)
    for c, spectra in enumerate(transform_blocks(dft_table, data, freq_count, halves, chunks)):
        sent = (spectra * LINK_SCALE).astype(jnp.float16)
        received = lax.all_to_all(sent, "tm", split_axis=0, concat_axis=0, tiled=True)
        high, low = split_pair(received.astype(jnp.float32))
        pieces.append((high, low))
        part_weights = split_weights[:, c * width:(c + 1) * width]
        partial_square = gram_call(high, low, part_weights, width, 2 * local_blocks)
        square = partial_square if square is None else square + partial_square
    recv_rows = pieces[0][0].shape[0]
    square = square * (1.0 / (LINK_SCALE * LINK_SCALE * total_points))
    natural = jnp.arange(rows, dtype=jnp.int32)
    part, block = natural // block_count, natural % block_count
    group = 2 * local_blocks
    home = (block // local_blocks) * (group * halves) + part * local_blocks + block % local_blocks
    recv_index = jnp.arange(recv_rows, dtype=jnp.int32)
    pick = [(recv_index[None, :] == (home + h * group)[:, None]).astype(jnp.float32) for h in range(halves)]
    row_half = recv_index // group % halves
    same_half = row_half[:, None] == row_half[None, :]
    either = pick[0] + pick[1]
    square = jnp.where(same_half, square, jnp.zeros_like(square))
    square = jnp.dot(jnp.dot(either, square, precision=HIGH), either.T, precision=HIGH)
    g_one = square[:block_count, :block_count] + square[block_count:, block_count:]
    g_two = square[:block_count, block_count:] - square[block_count:, :block_count]
    lower = jnp.arange(block_count)[:, None] > jnp.arange(block_count)[None, :]
    packed = jnp.where(lower, g_two, g_one)
    rows_half = block_count // 2
    packed = jnp.concatenate([packed[:rows_half], packed[rows_half:]], axis=1)
    spread = jnp.broadcast_to(packed[None], (space_count,) + packed.shape)
    partials = lax.all_to_all(spread, "space", split_axis=0, concat_axis=0, tiled=True)
    total = partials[0]
    for source in range(1, space_count):
        total = total + partials[source]
    total = jnp.concatenate([total[:, :block_count], total[:, block_count:]], axis=0)
    upper = jnp.where(lower, jnp.zeros_like(total), total)
    strict = jnp.where(lower, total, jnp.zeros_like(total))
    g_one = upper + jnp.where(lower, upper.T, jnp.zeros_like(total))
    g_two = strict - strict.T

    embedded = jnp.concatenate(
        [jnp.concatenate([g_one, -g_two], axis=1), jnp.concatenate([g_two, g_one], axis=1)], axis=0
    )
    inv_root = inverse_root(embedded)
    z_top = inv_root[:block_count, :block_count]
    z_low = inv_root[block_count:, :block_count]
    coeff = jnp.concatenate(
        [jnp.concatenate([z_top.T, -z_low.T], axis=1), jnp.concatenate([z_low.T, z_top.T], axis=1)],
        axis=0,
    )
    kept_count = lax.dynamic_slice_in_dim(n_keep, lax.axis_index("tm"), 1)
    kept_rows = jnp.arange(rows, dtype=jnp.int32) % block_count < kept_count
    coeff = jnp.where(kept_rows[:, None], coeff, jnp.zeros_like(coeff)) * (1.0 / LINK_SCALE)
    coeff_halves = jnp.stack([jnp.dot(coeff, p, precision=HIGH) for p in pick])
    mode_field = mode_call(coeff_halves, pieces).reshape(1, 2, block_count, points_here)
    energy = (jnp.trace(g_one) / block_count).reshape(1)
    return (mode_field, energy)


def solution(mesh):
    placed = (P("tm", "space"), P("space"), P(), P())
    return jax.shard_map(
        shards,
        mesh=mesh,
        in_specs=placed,
        out_specs=(P("tm", None, None, "space"), P("tm")),
        check_vma=False,
    )
```

```python
import functools

import jax
import jax.numpy as jnp
from jax import lax
from jax.sharding import PartitionSpec as P
from jax.experimental import pallas as pl
from jax.experimental.pallas import tpu as pltpu

NT = 64
NS_STEPS = 4
HIGH = lax.Precision.HIGHEST
LINK_SCALE = 128.0


def spectra_table(freqs):
    time_int = jnp.arange(NT, dtype=jnp.int32)
    time_float = time_int.astype(jnp.float32)
    window = 0.5 - 0.5 * jnp.cos(2.0 * jnp.pi * time_float / NT)
    norm = jnp.sqrt(jnp.sum(window * window))
    wrapped = freqs[:, None] * time_int[None, :] % NT
    phase_angle = 2.0 * jnp.pi * wrapped.astype(jnp.float32) / NT
    real_rows = window[None, :] * jnp.cos(phase_angle) / norm
    imag_rows = -window[None, :] * jnp.sin(phase_angle) / norm
    return jnp.concatenate([real_rows, imag_rows], axis=0).astype(jnp.bfloat16)


def transform_blocks(dft_table, snapshots, freq_count, halves):
    local_blocks = snapshots.shape[0] // NT
    points = snapshots.shape[1] // halves
    table_view = dft_table.reshape(2, freq_count, NT).transpose(1, 0, 2)
    chooser = jnp.eye(local_blocks, dtype=dft_table.dtype)
    halver = jnp.eye(halves, dtype=dft_table.dtype)
    lifted = (
        table_view[:, None, :, None, None, None, :]
        * halver[None, :, None, None, :, None, None]
        * chooser[None, None, None, :, None, :, None]
    )
    lifted = lifted.reshape(freq_count * halves * 2 * local_blocks, halves * local_blocks * NT)
    stacked = jnp.concatenate([snapshots[:, h * points:(h + 1) * points] for h in range(halves)], axis=0)
    return jnp.dot(lifted, stacked, preferred_element_type=jnp.float32)


def split_pair(value):
    rounded = lax.reduce_precision(value, exponent_bits=8, mantissa_bits=7)
    return rounded.astype(jnp.bfloat16), (value - rounded).astype(jnp.bfloat16)


NT_DIMS = (((1,), (1,)), ((), ()))


def gram_kernel(group, x_ref, w_ref, o_ref):
    @pl.when(pl.program_id(0) == 0)
    def _():
        o_ref[...] = jnp.zeros_like(o_ref)

    x = x_ref[...]
    x_hi, x_lo = split_pair(x)
    odd = lax.broadcasted_iota(jnp.int32, x.shape, 0) // group % 2 == 1
    row_weights = jnp.where(odd, w_ref[1:2, :], w_ref[0:1, :])
    y_hi, y_lo = split_pair(x * row_weights)
    acc = lax.dot_general(x_hi, y_hi, NT_DIMS, preferred_element_type=jnp.float32)
    acc += lax.dot_general(x_lo, y_hi, NT_DIMS, preferred_element_type=jnp.float32)
    acc += lax.dot_general(x_hi, y_lo, NT_DIMS, preferred_element_type=jnp.float32)
    o_ref[...] += acc


def gram_call(values, weights, chunk, group):
    rows, points = values.shape
    return pl.pallas_call(
        functools.partial(gram_kernel, group),
        grid=(points // chunk,),
        in_specs=[
            pl.BlockSpec((rows, chunk), lambda k: (0, k)),
            pl.BlockSpec((2, chunk), lambda k: (0, k)),
        ],
        compiler_params=pltpu.CompilerParams(allow_input_fusion=[True, False]),
        out_specs=pl.BlockSpec((rows, rows), lambda k: (0, 0)),
        out_shape=jax.ShapeDtypeStruct((rows, rows), jnp.float32),
        cost_estimate=pl.CostEstimate(
            flops=6 * rows * rows * points, transcendentals=0, bytes_accessed=4 * rows * points
        ),
    )(values, weights.reshape(2, points))


def mode_kernel(c_hi_ref, c_lo_ref, hi_ref, lo_ref, o_ref):
    x_hi = hi_ref[...]
    x_lo = lo_ref[...]
    c_hi = c_hi_ref[...]
    acc = jnp.dot(c_hi, x_hi, preferred_element_type=jnp.float32)
    acc += jnp.dot(c_lo_ref[...], x_hi, preferred_element_type=jnp.float32)
    acc += jnp.dot(c_hi, x_lo, preferred_element_type=jnp.float32)
    o_ref[...] = acc.astype(o_ref.dtype)


def mode_call(coeff_halves, high, low, chunk):
    halves, out_rows, rows = coeff_halves.shape
    points = high.shape[1]
    steps = points // chunk
    c_hi, c_lo = split_pair(coeff_halves)
    return pl.pallas_call(
        mode_kernel,
        grid=(steps, halves),
        in_specs=[
            pl.BlockSpec((None, out_rows, rows), lambda k, h: (h, 0, 0)),
            pl.BlockSpec((None, out_rows, rows), lambda k, h: (h, 0, 0)),
            pl.BlockSpec((rows, chunk), lambda k, h: (0, k)),
            pl.BlockSpec((rows, chunk), lambda k, h: (0, k)),
        ],
        out_specs=pl.BlockSpec((out_rows, chunk), lambda k, h: (0, h * steps + k)),
        out_shape=jax.ShapeDtypeStruct((out_rows, halves * points), jnp.bfloat16),
        cost_estimate=pl.CostEstimate(
            flops=6 * out_rows * rows * points * halves,
            transcendentals=0,
            bytes_accessed=4 * rows * points * halves + 2 * out_rows * points * halves,
        ),
    )(c_hi, c_lo, high, low)


def butterfly_sum(value, axis, size):
    step = 1
    while step < size:
        pairs = [(i, i ^ step) for i in range(size)]
        value = value + lax.ppermute(value, axis, pairs)
        step *= 2
    return value


def inverse_root(embedded):
    size_two = embedded.shape[0]
    frobenius = jnp.sqrt(jnp.sum(embedded * embedded) + 1e-06)
    identity = jnp.eye(size_two, dtype=jnp.float32)
    current = embedded / frobenius
    factor = 1.5 * identity - 0.5 * current
    current = jnp.dot(current, factor, precision=HIGH)
    result = factor
    for sweep in range(1, NS_STEPS):
        factor = 1.5 * identity - 0.5 * jnp.dot(result, current, precision=HIGH)
        current = jnp.dot(current, factor, precision=HIGH)
        result = jnp.dot(factor, result, precision=HIGH)
    return result


def shards(data, weights, freqs, n_keep):
    tm_count = lax.axis_size("tm")
    space_count = lax.axis_size("space")
    freq_count = freqs.shape[0]
    points_here = data.shape[1]
    total_points = points_here * space_count
    local_blocks = data.shape[0] // NT
    block_count = local_blocks * tm_count
    rows = 2 * block_count

    dft_table = spectra_table(freqs)
    halves = 2
    spectra = transform_blocks(dft_table, data, freq_count, halves)
    sent = (spectra * LINK_SCALE).astype(jnp.float16)
    received = lax.all_to_all(sent, "tm", split_axis=0, concat_axis=0, tiled=True)
    values = received.astype(jnp.float32)
    high, low = split_pair(values)
    recv_rows = received.shape[0]

    square = gram_call(values, weights, 2048, 2 * local_blocks) * (1.0 / (LINK_SCALE * LINK_SCALE * total_points))
    natural = jnp.arange(rows, dtype=jnp.int32)
    part, block = natural // block_count, natural % block_count
    group = 2 * local_blocks
    home = (block // local_blocks) * (group * halves) + part * local_blocks + block % local_blocks
    recv_index = jnp.arange(recv_rows, dtype=jnp.int32)
    pick = [(recv_index[None, :] == (home + h * group)[:, None]).astype(jnp.float32) for h in range(halves)]
    row_half = recv_index // group % halves
    same_half = row_half[:, None] == row_half[None, :]
    either = pick[0] + pick[1]
    square = jnp.where(same_half, square, jnp.zeros_like(square))
    square = jnp.dot(jnp.dot(either, square, precision=HIGH), either.T, precision=HIGH)
    g_one = square[:block_count, :block_count] + square[block_count:, block_count:]
    g_two = square[:block_count, block_count:] - square[block_count:, :block_count]
    lower = jnp.arange(block_count)[:, None] > jnp.arange(block_count)[None, :]
    packed = jnp.where(lower, g_two, g_one)
    rows_half = block_count // 2
    packed = jnp.concatenate([packed[:rows_half], packed[rows_half:]], axis=1)
    spread = jnp.broadcast_to(packed[None], (space_count,) + packed.shape)
    partials = lax.all_to_all(spread, "space", split_axis=0, concat_axis=0, tiled=True)
    total = partials[0]
    for source in range(1, space_count):
        total = total + partials[source]
    total = jnp.concatenate([total[:, :block_count], total[:, block_count:]], axis=0)
    upper = jnp.where(lower, jnp.zeros_like(total), total)
    strict = jnp.where(lower, total, jnp.zeros_like(total))
    g_one = upper + jnp.where(lower, upper.T, jnp.zeros_like(total))
    g_two = strict - strict.T

    embedded = jnp.concatenate(
        [jnp.concatenate([g_one, -g_two], axis=1), jnp.concatenate([g_two, g_one], axis=1)], axis=0
    )
    inv_root = inverse_root(embedded)
    z_top = inv_root[:block_count, :block_count]
    z_low = inv_root[block_count:, :block_count]
    coeff = jnp.concatenate(
        [jnp.concatenate([z_top.T, -z_low.T], axis=1), jnp.concatenate([z_low.T, z_top.T], axis=1)],
        axis=0,
    )
    kept_count = lax.dynamic_slice_in_dim(n_keep, lax.axis_index("tm"), 1)
    kept_rows = jnp.arange(rows, dtype=jnp.int32) % block_count < kept_count
    coeff = jnp.where(kept_rows[:, None], coeff, jnp.zeros_like(coeff)) * (1.0 / LINK_SCALE)
    coeff_halves = jnp.stack([jnp.dot(coeff, p, precision=HIGH) for p in pick])
    mode_field = mode_call(coeff_halves, high, low, 2048).reshape(1, 2, block_count, points_here)
    energy = (jnp.trace(g_one) / block_count).reshape(1)
    return (mode_field, energy)


def solution(mesh):
    placed = (P("tm", "space"), P("space"), P(), P())
    return jax.shard_map(
        shards,
        mesh=mesh,
        in_specs=placed,
        out_specs=(P("tm", None, None, "space"), P("tm")),
        check_vma=False,
    )
```

```python
import functools

import jax
import jax.numpy as jnp
from jax import lax
from jax.sharding import PartitionSpec as P
from jax.experimental import pallas as pl
from jax.experimental.pallas import tpu as pltpu

NT = 64
NS_STEPS = 4
HIGH = lax.Precision.HIGHEST
LINK_SCALE = 128.0


def spectra_table(freqs):
    time_int = jnp.arange(NT, dtype=jnp.int32)
    time_float = time_int.astype(jnp.float32)
    window = 0.5 - 0.5 * jnp.cos(2.0 * jnp.pi * time_float / NT)
    norm = jnp.sqrt(jnp.sum(window * window))
    wrapped = freqs[:, None] * time_int[None, :] % NT
    phase_angle = 2.0 * jnp.pi * wrapped.astype(jnp.float32) / NT
    real_rows = window[None, :] * jnp.cos(phase_angle) / norm
    imag_rows = -window[None, :] * jnp.sin(phase_angle) / norm
    return jnp.concatenate([real_rows, imag_rows], axis=0).astype(jnp.bfloat16)


def transform_blocks(dft_table, snapshots, freq_count, halves):
    local_blocks = snapshots.shape[0] // NT
    points = snapshots.shape[1] // halves
    table_view = dft_table.reshape(2, freq_count, NT).transpose(1, 0, 2)
    chooser = jnp.eye(local_blocks, dtype=dft_table.dtype)
    halver = jnp.eye(halves, dtype=dft_table.dtype)
    lifted = (
        table_view[:, None, :, None, None, None, :]
        * halver[None, :, None, None, :, None, None]
        * chooser[None, None, None, :, None, :, None]
    )
    lifted = lifted.reshape(freq_count * halves * 2 * local_blocks, halves * local_blocks * NT)
    stacked = jnp.concatenate([snapshots[:, h * points:(h + 1) * points] for h in range(halves)], axis=0)
    return jnp.dot(lifted, stacked, preferred_element_type=jnp.float32)


def split_pair(value):
    rounded = lax.reduce_precision(value, exponent_bits=8, mantissa_bits=7)
    return rounded.astype(jnp.bfloat16), (value - rounded).astype(jnp.bfloat16)


NT_DIMS = (((1,), (1,)), ((), ()))


def gram_kernel(group, x_ref, w_ref, o_ref):
    @pl.when(pl.program_id(0) == 0)
    def _():
        o_ref[...] = jnp.zeros_like(o_ref)

    x = x_ref[...]
    x_hi, x_lo = split_pair(x)
    odd = lax.broadcasted_iota(jnp.int32, x.shape, 0) // group % 2 == 1
    row_weights = jnp.where(odd, w_ref[1:2, :], w_ref[0:1, :])
    y_hi, y_lo = split_pair(x * row_weights)
    acc = lax.dot_general(x_hi, y_hi, NT_DIMS, preferred_element_type=jnp.float32)
    acc += lax.dot_general(x_lo, y_hi, NT_DIMS, preferred_element_type=jnp.float32)
    acc += lax.dot_general(x_hi, y_lo, NT_DIMS, preferred_element_type=jnp.float32)
    o_ref[...] += acc


def gram_call(values, weights, chunk, group):
    rows, points = values.shape
    return pl.pallas_call(
        functools.partial(gram_kernel, group),
        grid=(points // chunk,),
        in_specs=[
            pl.BlockSpec((rows, chunk), lambda k: (0, k)),
            pl.BlockSpec((2, chunk), lambda k: (0, k)),
        ],
        compiler_params=pltpu.CompilerParams(allow_input_fusion=[True, False]),
        out_specs=pl.BlockSpec((rows, rows), lambda k: (0, 0)),
        out_shape=jax.ShapeDtypeStruct((rows, rows), jnp.float32),
        cost_estimate=pl.CostEstimate(
            flops=6 * rows * rows * points, transcendentals=0, bytes_accessed=4 * rows * points
        ),
    )(values, weights.reshape(2, points))


def mode_kernel(c_hi_ref, c_lo_ref, hi_ref, lo_ref, o_ref):
    x_hi = hi_ref[...]
    x_lo = lo_ref[...]
    c_hi = c_hi_ref[...]
    acc = jnp.dot(c_hi, x_hi, preferred_element_type=jnp.float32)
    acc += jnp.dot(c_lo_ref[...], x_hi, preferred_element_type=jnp.float32)
    acc += jnp.dot(c_hi, x_lo, preferred_element_type=jnp.float32)
    o_ref[...] = acc.astype(o_ref.dtype)


def mode_call(coeff_halves, high, low, chunk):
    halves, out_rows, rows = coeff_halves.shape
    points = high.shape[1]
    steps = points // chunk
    c_hi, c_lo = split_pair(coeff_halves)
    return pl.pallas_call(
        mode_kernel,
        grid=(steps, halves),
        in_specs=[
            pl.BlockSpec((None, out_rows, rows), lambda k, h: (h, 0, 0)),
            pl.BlockSpec((None, out_rows, rows), lambda k, h: (h, 0, 0)),
            pl.BlockSpec((rows, chunk), lambda k, h: (0, k)),
            pl.BlockSpec((rows, chunk), lambda k, h: (0, k)),
        ],
        out_specs=pl.BlockSpec((out_rows, chunk), lambda k, h: (0, h * steps + k)),
        out_shape=jax.ShapeDtypeStruct((out_rows, halves * points), jnp.bfloat16),
        cost_estimate=pl.CostEstimate(
            flops=6 * out_rows * rows * points * halves,
            transcendentals=0,
            bytes_accessed=4 * rows * points * halves + 2 * out_rows * points * halves,
        ),
    )(c_hi, c_lo, high, low)


def butterfly_sum(value, axis, size):
    step = 1
    while step < size:
        pairs = [(i, i ^ step) for i in range(size)]
        value = value + lax.ppermute(value, axis, pairs)
        step *= 2
    return value


def inverse_root(embedded):
    size_two = embedded.shape[0]
    frobenius = jnp.sqrt(jnp.sum(embedded * embedded) + 1e-06)
    identity = jnp.eye(size_two, dtype=jnp.float32)
    current = embedded / frobenius
    factor = 1.5 * identity - 0.5 * current
    current = jnp.dot(current, factor, precision=HIGH)
    result = factor
    for sweep in range(1, NS_STEPS):
        factor = 1.5 * identity - 0.5 * jnp.dot(result, current, precision=HIGH)
        current = jnp.dot(current, factor, precision=HIGH)
        result = jnp.dot(factor, result, precision=HIGH)
    return result


def shards(data, weights, freqs, n_keep):
    tm_count = lax.axis_size("tm")
    space_count = lax.axis_size("space")
    freq_count = freqs.shape[0]
    points_here = data.shape[1]
    total_points = points_here * space_count
    local_blocks = data.shape[0] // NT
    block_count = local_blocks * tm_count
    rows = 2 * block_count

    dft_table = spectra_table(freqs)
    halves = 2
    spectra = transform_blocks(dft_table, data, freq_count, halves)
    sent = (spectra * LINK_SCALE).astype(jnp.float16)
    received = lax.all_to_all(sent, "tm", split_axis=0, concat_axis=0, tiled=True)
    values = received.astype(jnp.float32)
    high, low = split_pair(values)
    recv_rows = received.shape[0]

    square = gram_call(values, weights, 2048, 2 * local_blocks) * (1.0 / (LINK_SCALE * LINK_SCALE * total_points))
    natural = jnp.arange(rows, dtype=jnp.int32)
    part, block = natural // block_count, natural % block_count
    group = 2 * local_blocks
    home = (block // local_blocks) * (group * halves) + part * local_blocks + block % local_blocks
    recv_index = jnp.arange(recv_rows, dtype=jnp.int32)
    pick = [(recv_index[None, :] == (home + h * group)[:, None]).astype(jnp.float32) for h in range(halves)]
    row_half = recv_index // group % halves
    same_half = row_half[:, None] == row_half[None, :]
    either = pick[0] + pick[1]
    square = jnp.where(same_half, square, jnp.zeros_like(square))
    square = jnp.dot(jnp.dot(either, square, precision=HIGH), either.T, precision=HIGH)
    g_one = square[:block_count, :block_count] + square[block_count:, block_count:]
    g_two = square[:block_count, block_count:] - square[block_count:, :block_count]
    lower = jnp.arange(block_count)[:, None] > jnp.arange(block_count)[None, :]
    packed = jnp.where(lower, g_two, g_one)
    rows_half = block_count // 2
    packed = jnp.concatenate([packed[:rows_half], packed[rows_half:]], axis=1)
    spread = jnp.broadcast_to(packed[None], (space_count,) + packed.shape)
    partials = lax.all_to_all(spread, "space", split_axis=0, concat_axis=0, tiled=True)
    total = partials[0]
    for source in range(1, space_count):
        total = total + partials[source]
    total = jnp.concatenate([total[:, :block_count], total[:, block_count:]], axis=0)
    flipped = lax.dot_general(
        jnp.eye(block_count, dtype=jnp.float32), total, NT_DIMS, precision=HIGH
    )
    above = jnp.arange(block_count)[:, None] < jnp.arange(block_count)[None, :]
    g_one = jnp.where(lower, flipped, total)
    g_two = jnp.where(lower, total, jnp.where(above, -flipped, jnp.zeros_like(total)))

    embedded = jnp.concatenate(
        [jnp.concatenate([g_one, -g_two], axis=1), jnp.concatenate([g_two, g_one], axis=1)], axis=0
    )
    inv_root = inverse_root(embedded)
    z_top = inv_root[:block_count, :block_count]
    z_low = inv_root[block_count:, :block_count]
    coeff = jnp.concatenate(
        [jnp.concatenate([z_top.T, -z_low.T], axis=1), jnp.concatenate([z_low.T, z_top.T], axis=1)],
        axis=0,
    )
    kept_count = lax.dynamic_slice_in_dim(n_keep, lax.axis_index("tm"), 1)
    kept_rows = jnp.arange(rows, dtype=jnp.int32) % block_count < kept_count
    coeff = jnp.where(kept_rows[:, None], coeff, jnp.zeros_like(coeff)) * (1.0 / LINK_SCALE)
    coeff_halves = jnp.stack([jnp.dot(coeff, p, precision=HIGH) for p in pick])
    mode_field = mode_call(coeff_halves, high, low, 2048).reshape(1, 2, block_count, points_here)
    energy = (jnp.trace(g_one) / block_count).reshape(1)
    return (mode_field, energy)


def solution(mesh):
    placed = (P("tm", "space"), P("space"), P(), P())
    return jax.shard_map(
        shards,
        mesh=mesh,
        in_specs=placed,
        out_specs=(P("tm", None, None, "space"), P("tm")),
        check_vma=False,
    )
```

```python
import functools

import jax
import jax.numpy as jnp
from jax import lax
from jax.sharding import PartitionSpec as P
from jax.experimental import pallas as pl
from jax.experimental.pallas import tpu as pltpu

NT = 64
NS_STEPS = 4
HIGH = lax.Precision.HIGHEST
LINK_SCALE = 128.0


def spectra_table(freqs):
    time_int = jnp.arange(NT, dtype=jnp.int32)
    time_float = time_int.astype(jnp.float32)
    window = 0.5 - 0.5 * jnp.cos(2.0 * jnp.pi * time_float / NT)
    norm = jnp.sqrt(jnp.sum(window * window))
    wrapped = freqs[:, None] * time_int[None, :] % NT
    phase_angle = 2.0 * jnp.pi * wrapped.astype(jnp.float32) / NT
    real_rows = window[None, :] * jnp.cos(phase_angle) / norm
    imag_rows = -window[None, :] * jnp.sin(phase_angle) / norm
    return jnp.concatenate([real_rows, imag_rows], axis=0).astype(jnp.bfloat16)


def transform_blocks(dft_table, snapshots, freq_count, halves):
    local_blocks = snapshots.shape[0] // NT
    points = snapshots.shape[1] // halves
    table_view = dft_table.reshape(2, freq_count, NT).transpose(1, 0, 2)
    chooser = jnp.eye(local_blocks, dtype=dft_table.dtype)
    halver = jnp.eye(halves, dtype=dft_table.dtype)
    lifted = (
        table_view[:, None, :, None, None, None, :]
        * halver[None, :, None, None, :, None, None]
        * chooser[None, None, None, :, None, :, None]
    )
    lifted = lifted.reshape(freq_count * halves * 2 * local_blocks, halves * local_blocks * NT)
    stacked = jnp.concatenate([snapshots[:, h * points:(h + 1) * points] for h in range(halves)], axis=0)
    return jnp.dot(lifted, stacked, preferred_element_type=jnp.float32)


def split_pair(value):
    rounded = lax.reduce_precision(value, exponent_bits=8, mantissa_bits=7)
    return rounded.astype(jnp.bfloat16), (value - rounded).astype(jnp.bfloat16)


NT_DIMS = (((1,), (1,)), ((), ()))


def gram_kernel(group, x_ref, w_ref, o_ref):
    @pl.when(pl.program_id(0) == 0)
    def _():
        o_ref[...] = jnp.zeros_like(o_ref)

    x = x_ref[...]
    x_hi, x_lo = split_pair(x)
    odd = lax.broadcasted_iota(jnp.int32, x.shape, 0) // group % 2 == 1
    row_weights = jnp.where(odd, w_ref[1:2, :], w_ref[0:1, :])
    y_hi, y_lo = split_pair(x * row_weights)
    acc = lax.dot_general(x_hi, y_hi, NT_DIMS, preferred_element_type=jnp.float32)
    acc += lax.dot_general(x_lo, y_hi, NT_DIMS, preferred_element_type=jnp.float32)
    acc += lax.dot_general(x_hi, y_lo, NT_DIMS, preferred_element_type=jnp.float32)
    o_ref[...] += acc


def gram_call(values, weights, chunk, group):
    rows, points = values.shape
    return pl.pallas_call(
        functools.partial(gram_kernel, group),
        grid=(points // chunk,),
        in_specs=[
            pl.BlockSpec((rows, chunk), lambda k: (0, k)),
            pl.BlockSpec((2, chunk), lambda k: (0, k)),
        ],
        compiler_params=pltpu.CompilerParams(allow_input_fusion=[True, False]),
        out_specs=pl.BlockSpec((rows, rows), lambda k: (0, 0)),
        out_shape=jax.ShapeDtypeStruct((rows, rows), jnp.float32),
        cost_estimate=pl.CostEstimate(
            flops=6 * rows * rows * points, transcendentals=0, bytes_accessed=4 * rows * points
        ),
    )(values, weights.reshape(2, points))


def mode_kernel(c_hi_ref, c_lo_ref, x_ref, o_ref):
    x_hi, x_lo = split_pair(x_ref[...])
    c_hi = c_hi_ref[...]
    acc = jnp.dot(c_hi, x_hi, preferred_element_type=jnp.float32)
    acc += jnp.dot(c_lo_ref[...], x_hi, preferred_element_type=jnp.float32)
    acc += jnp.dot(c_hi, x_lo, preferred_element_type=jnp.float32)
    o_ref[...] = acc.astype(o_ref.dtype)


def mode_call(coeff_halves, values, chunk):
    halves, out_rows, rows = coeff_halves.shape
    points = values.shape[1]
    steps = points // chunk
    c_hi, c_lo = split_pair(coeff_halves)
    return pl.pallas_call(
        mode_kernel,
        grid=(steps, halves),
        in_specs=[
            pl.BlockSpec((None, out_rows, rows), lambda k, h: (h, 0, 0)),
            pl.BlockSpec((None, out_rows, rows), lambda k, h: (h, 0, 0)),
            pl.BlockSpec((rows, chunk), lambda k, h: (0, k)),
        ],
        out_specs=pl.BlockSpec((out_rows, chunk), lambda k, h: (0, h * steps + k)),
        out_shape=jax.ShapeDtypeStruct((out_rows, halves * points), jnp.bfloat16),
        compiler_params=pltpu.CompilerParams(allow_input_fusion=[False, False, True]),
        cost_estimate=pl.CostEstimate(
            flops=6 * out_rows * rows * points * halves,
            transcendentals=0,
            bytes_accessed=4 * rows * points * halves + 2 * out_rows * points * halves,
        ),
    )(c_hi, c_lo, values)


def butterfly_sum(value, axis, size):
    step = 1
    while step < size:
        pairs = [(i, i ^ step) for i in range(size)]
        value = value + lax.ppermute(value, axis, pairs)
        step *= 2
    return value


def inverse_root(embedded):
    size_two = embedded.shape[0]
    frobenius = jnp.sqrt(jnp.sum(embedded * embedded) + 1e-06)
    identity = jnp.eye(size_two, dtype=jnp.float32)
    current = embedded / frobenius
    factor = 1.5 * identity - 0.5 * current
    current = jnp.dot(current, factor, precision=HIGH)
    result = factor
    for sweep in range(1, NS_STEPS):
        factor = 1.5 * identity - 0.5 * jnp.dot(result, current, precision=HIGH)
        current = jnp.dot(current, factor, precision=HIGH)
        result = jnp.dot(factor, result, precision=HIGH)
    return result


def shards(data, weights, freqs, n_keep):
    tm_count = lax.axis_size("tm")
    space_count = lax.axis_size("space")
    freq_count = freqs.shape[0]
    points_here = data.shape[1]
    total_points = points_here * space_count
    local_blocks = data.shape[0] // NT
    block_count = local_blocks * tm_count
    rows = 2 * block_count

    dft_table = spectra_table(freqs)
    halves = 2
    spectra = transform_blocks(dft_table, data, freq_count, halves)
    sent = (spectra * LINK_SCALE).astype(jnp.float16)
    received = lax.all_to_all(sent, "tm", split_axis=0, concat_axis=0, tiled=True)
    values = received.astype(jnp.float32)
    recv_rows = received.shape[0]

    square = gram_call(values, weights, 2048, 2 * local_blocks) * (1.0 / (LINK_SCALE * LINK_SCALE * total_points))
    natural = jnp.arange(rows, dtype=jnp.int32)
    part, block = natural // block_count, natural % block_count
    group = 2 * local_blocks
    home = (block // local_blocks) * (group * halves) + part * local_blocks + block % local_blocks
    recv_index = jnp.arange(recv_rows, dtype=jnp.int32)
    pick = [(recv_index[None, :] == (home + h * group)[:, None]).astype(jnp.float32) for h in range(halves)]
    row_half = recv_index // group % halves
    same_half = row_half[:, None] == row_half[None, :]
    either = pick[0] + pick[1]
    square = jnp.where(same_half, square, jnp.zeros_like(square))
    square = jnp.dot(jnp.dot(either, square, precision=HIGH), either.T, precision=HIGH)
    g_one = square[:block_count, :block_count] + square[block_count:, block_count:]
    g_two = square[:block_count, block_count:] - square[block_count:, :block_count]
    lower = jnp.arange(block_count)[:, None] > jnp.arange(block_count)[None, :]
    packed = jnp.where(lower, g_two, g_one)
    rows_half = block_count // 2
    packed = jnp.concatenate([packed[:rows_half], packed[rows_half:]], axis=1)
    spread = jnp.broadcast_to(packed[None], (space_count,) + packed.shape)
    partials = lax.all_to_all(spread, "space", split_axis=0, concat_axis=0, tiled=True)
    total = partials[0]
    for source in range(1, space_count):
        total = total + partials[source]
    total = jnp.concatenate([total[:, :block_count], total[:, block_count:]], axis=0)
    flipped = lax.dot_general(
        jnp.eye(block_count, dtype=jnp.float32), total, NT_DIMS, precision=HIGH
    )
    above = jnp.arange(block_count)[:, None] < jnp.arange(block_count)[None, :]
    g_one = jnp.where(lower, flipped, total)
    g_two = jnp.where(lower, total, jnp.where(above, -flipped, jnp.zeros_like(total)))

    embedded = jnp.concatenate(
        [jnp.concatenate([g_one, -g_two], axis=1), jnp.concatenate([g_two, g_one], axis=1)], axis=0
    )
    inv_root = inverse_root(embedded)
    z_top = inv_root[:block_count, :block_count]
    z_low = inv_root[block_count:, :block_count]
    coeff = jnp.concatenate(
        [jnp.concatenate([z_top.T, -z_low.T], axis=1), jnp.concatenate([z_low.T, z_top.T], axis=1)],
        axis=0,
    )
    kept_count = lax.dynamic_slice_in_dim(n_keep, lax.axis_index("tm"), 1)
    kept_rows = jnp.arange(rows, dtype=jnp.int32) % block_count < kept_count
    coeff = jnp.where(kept_rows[:, None], coeff, jnp.zeros_like(coeff)) * (1.0 / LINK_SCALE)
    coeff_halves = jnp.stack([jnp.dot(coeff, p, precision=HIGH) for p in pick])
    mode_field = mode_call(coeff_halves, values, 2048).reshape(1, 2, block_count, points_here)
    energy = (jnp.trace(g_one) / block_count).reshape(1)
    return (mode_field, energy)


def solution(mesh):
    placed = (P("tm", "space"), P("space"), P(), P())
    return jax.shard_map(
        shards,
        mesh=mesh,
        in_specs=placed,
        out_specs=(P("tm", None, None, "space"), P("tm")),
        check_vma=False,
    )
```

```python
import functools

import jax
import jax.numpy as jnp
from jax import lax
from jax.sharding import PartitionSpec as P
from jax.experimental import pallas as pl
from jax.experimental.pallas import tpu as pltpu

NT = 64
NS_STEPS = 4
HIGH = lax.Precision.HIGHEST
LINK_SCALE = 128.0


def spectra_table(freqs):
    time_int = jnp.arange(NT, dtype=jnp.int32)
    time_float = time_int.astype(jnp.float32)
    window = 0.5 - 0.5 * jnp.cos(2.0 * jnp.pi * time_float / NT)
    norm = jnp.sqrt(jnp.sum(window * window))
    wrapped = freqs[:, None] * time_int[None, :] % NT
    phase_angle = 2.0 * jnp.pi * wrapped.astype(jnp.float32) / NT
    real_rows = window[None, :] * jnp.cos(phase_angle) / norm
    imag_rows = -window[None, :] * jnp.sin(phase_angle) / norm
    return jnp.concatenate([real_rows, imag_rows], axis=0).astype(jnp.bfloat16)


def transform_blocks(dft_table, snapshots, freq_count, halves):
    local_blocks = snapshots.shape[0] // NT
    points = snapshots.shape[1] // halves
    table_view = dft_table.reshape(2, freq_count, NT).transpose(1, 0, 2)
    chooser = jnp.eye(local_blocks, dtype=dft_table.dtype)
    halver = jnp.eye(halves, dtype=dft_table.dtype)
    lifted = (
        table_view[:, None, :, None, None, None, :]
        * halver[None, :, None, None, :, None, None]
        * chooser[None, None, None, :, None, :, None]
    )
    lifted = lifted.reshape(freq_count * halves * 2 * local_blocks, halves * local_blocks * NT)
    stacked = jnp.concatenate([snapshots[:, h * points:(h + 1) * points] for h in range(halves)], axis=0)
    return jnp.dot(lifted, stacked, preferred_element_type=jnp.float32)


def split_pair(value):
    rounded = lax.reduce_precision(value, exponent_bits=8, mantissa_bits=7)
    return rounded.astype(jnp.bfloat16), (value - rounded).astype(jnp.bfloat16)


NT_DIMS = (((1,), (1,)), ((), ()))


def gram_kernel(group, x_ref, w_ref, o_ref):
    @pl.when(pl.program_id(0) == 0)
    def _():
        o_ref[...] = jnp.zeros_like(o_ref)

    x = x_ref[...]
    x_hi, x_lo = split_pair(x)
    odd = lax.broadcasted_iota(jnp.int32, x.shape, 0) // group % 2 == 1
    row_weights = jnp.where(odd, w_ref[1:2, :], w_ref[0:1, :])
    y_hi, y_lo = split_pair(x * row_weights)
    acc = lax.dot_general(x_hi, y_hi, NT_DIMS, preferred_element_type=jnp.float32)
    acc += lax.dot_general(x_lo, y_hi, NT_DIMS, preferred_element_type=jnp.float32)
    acc += lax.dot_general(x_hi, y_lo, NT_DIMS, preferred_element_type=jnp.float32)
    o_ref[...] += acc


def gram_call(values, weights, chunk, group):
    rows, points = values.shape
    return pl.pallas_call(
        functools.partial(gram_kernel, group),
        grid=(points // chunk,),
        in_specs=[
            pl.BlockSpec((rows, chunk), lambda k: (0, k)),
            pl.BlockSpec((2, chunk), lambda k: (0, k)),
        ],
        compiler_params=pltpu.CompilerParams(allow_input_fusion=[True, False]),
        out_specs=pl.BlockSpec((rows, rows), lambda k: (0, 0)),
        out_shape=jax.ShapeDtypeStruct((rows, rows), jnp.float32),
        cost_estimate=pl.CostEstimate(
            flops=6 * rows * rows * points, transcendentals=0, bytes_accessed=4 * rows * points
        ),
    )(values, weights.reshape(2, points))


def mode_kernel(c_hi_ref, c_lo_ref, x_ref, o_ref):
    x_hi, x_lo = split_pair(x_ref[...])
    c_hi = c_hi_ref[...]
    acc = jnp.dot(c_hi, x_hi, preferred_element_type=jnp.float32)
    acc += jnp.dot(c_lo_ref[...], x_hi, preferred_element_type=jnp.float32)
    acc += jnp.dot(c_hi, x_lo, preferred_element_type=jnp.float32)
    o_ref[...] = acc.astype(o_ref.dtype)


def mode_call(coeff_halves, values, chunk):
    halves, out_rows, rows = coeff_halves.shape
    points = values.shape[1]
    steps = points // chunk
    c_hi, c_lo = split_pair(coeff_halves)
    return pl.pallas_call(
        mode_kernel,
        grid=(steps, halves),
        in_specs=[
            pl.BlockSpec((None, out_rows, rows), lambda k, h: (h, 0, 0)),
            pl.BlockSpec((None, out_rows, rows), lambda k, h: (h, 0, 0)),
            pl.BlockSpec((rows, chunk), lambda k, h: (0, k)),
        ],
        out_specs=pl.BlockSpec((out_rows, chunk), lambda k, h: (0, h * steps + k)),
        out_shape=jax.ShapeDtypeStruct((out_rows, halves * points), jnp.bfloat16),
        compiler_params=pltpu.CompilerParams(allow_input_fusion=[False, False, True]),
        cost_estimate=pl.CostEstimate(
            flops=6 * out_rows * rows * points * halves,
            transcendentals=0,
            bytes_accessed=4 * rows * points * halves + 2 * out_rows * points * halves,
        ),
    )(c_hi, c_lo, values)


def butterfly_sum(value, axis, size):
    step = 1
    while step < size:
        pairs = [(i, i ^ step) for i in range(size)]
        value = value + lax.ppermute(value, axis, pairs)
        step *= 2
    return value


def inverse_root(embedded):
    size_two = embedded.shape[0]
    frobenius = jnp.sqrt(jnp.sum(embedded * embedded) + 1e-06)
    identity = jnp.eye(size_two, dtype=jnp.float32)
    current = embedded / frobenius
    factor = 1.5 * identity - 0.5 * current
    current = jnp.dot(current, factor, precision=HIGH)
    result = factor
    for sweep in range(1, NS_STEPS):
        factor = 1.5 * identity - 0.5 * jnp.dot(result, current, precision=HIGH)
        current = jnp.dot(current, factor, precision=HIGH)
        result = jnp.dot(factor, result, precision=HIGH)
    return result


def shards(data, weights, freqs, n_keep):
    tm_count = lax.axis_size("tm")
    space_count = lax.axis_size("space")
    freq_count = freqs.shape[0]
    points_here = data.shape[1]
    total_points = points_here * space_count
    local_blocks = data.shape[0] // NT
    block_count = local_blocks * tm_count
    rows = 2 * block_count

    dft_table = spectra_table(freqs)
    halves = 2
    spectra = transform_blocks(dft_table, data, freq_count, halves)
    sent = (spectra * LINK_SCALE).astype(jnp.float16)
    received = lax.all_to_all(sent, "tm", split_axis=0, concat_axis=0, tiled=True)
    values = received.astype(jnp.float32)
    recv_rows = received.shape[0]

    square = gram_call(values, weights, 1024, 2 * local_blocks) * (1.0 / (LINK_SCALE * LINK_SCALE * total_points))
    natural = jnp.arange(rows, dtype=jnp.int32)
    part, block = natural // block_count, natural % block_count
    group = 2 * local_blocks
    home = (block // local_blocks) * (group * halves) + part * local_blocks + block % local_blocks
    recv_index = jnp.arange(recv_rows, dtype=jnp.int32)
    pick = [(recv_index[None, :] == (home + h * group)[:, None]).astype(jnp.float32) for h in range(halves)]
    row_half = recv_index // group % halves
    same_half = row_half[:, None] == row_half[None, :]
    either = pick[0] + pick[1]
    square = jnp.where(same_half, square, jnp.zeros_like(square))
    square = jnp.dot(jnp.dot(either, square, precision=HIGH), either.T, precision=HIGH)
    g_one = square[:block_count, :block_count] + square[block_count:, block_count:]
    g_two = square[:block_count, block_count:] - square[block_count:, :block_count]
    lower = jnp.arange(block_count)[:, None] > jnp.arange(block_count)[None, :]
    packed = jnp.where(lower, g_two, g_one)
    rows_half = block_count // 2
    packed = jnp.concatenate([packed[:rows_half], packed[rows_half:]], axis=1)
    spread = jnp.broadcast_to(packed[None], (space_count,) + packed.shape)
    partials = lax.all_to_all(spread, "space", split_axis=0, concat_axis=0, tiled=True)
    total = partials[0]
    for source in range(1, space_count):
        total = total + partials[source]
    total = jnp.concatenate([total[:, :block_count], total[:, block_count:]], axis=0)
    flipped = lax.dot_general(
        jnp.eye(block_count, dtype=jnp.float32), total, NT_DIMS, precision=HIGH
    )
    above = jnp.arange(block_count)[:, None] < jnp.arange(block_count)[None, :]
    g_one = jnp.where(lower, flipped, total)
    g_two = jnp.where(lower, total, jnp.where(above, -flipped, jnp.zeros_like(total)))

    embedded = jnp.concatenate(
        [jnp.concatenate([g_one, -g_two], axis=1), jnp.concatenate([g_two, g_one], axis=1)], axis=0
    )
    inv_root = inverse_root(embedded)
    z_top = inv_root[:block_count, :block_count]
    z_low = inv_root[block_count:, :block_count]
    coeff = jnp.concatenate(
        [jnp.concatenate([z_top.T, -z_low.T], axis=1), jnp.concatenate([z_low.T, z_top.T], axis=1)],
        axis=0,
    )
    kept_count = lax.dynamic_slice_in_dim(n_keep, lax.axis_index("tm"), 1)
    kept_rows = jnp.arange(rows, dtype=jnp.int32) % block_count < kept_count
    coeff = jnp.where(kept_rows[:, None], coeff, jnp.zeros_like(coeff)) * (1.0 / LINK_SCALE)
    coeff_halves = jnp.stack([jnp.dot(coeff, p, precision=HIGH) for p in pick])
    mode_field = mode_call(coeff_halves, values, 1024).reshape(1, 2, block_count, points_here)
    energy = (jnp.trace(g_one) / block_count).reshape(1)
    return (mode_field, energy)


def solution(mesh):
    placed = (P("tm", "space"), P("space"), P(), P())
    return jax.shard_map(
        shards,
        mesh=mesh,
        in_specs=placed,
        out_specs=(P("tm", None, None, "space"), P("tm")),
        check_vma=False,
    )
```

```python
import functools

import jax
import jax.numpy as jnp
from jax import lax
from jax.sharding import PartitionSpec as P
from jax.experimental import pallas as pl
from jax.experimental.pallas import tpu as pltpu

NT = 64
NS_STEPS = 4
HIGH = lax.Precision.HIGHEST
LINK_SCALE = 128.0


def spectra_table(freqs):
    time_int = jnp.arange(NT, dtype=jnp.int32)
    time_float = time_int.astype(jnp.float32)
    window = 0.5 - 0.5 * jnp.cos(2.0 * jnp.pi * time_float / NT)
    norm = jnp.sqrt(jnp.sum(window * window))
    wrapped = freqs[:, None] * time_int[None, :] % NT
    phase_angle = 2.0 * jnp.pi * wrapped.astype(jnp.float32) / NT
    real_rows = window[None, :] * jnp.cos(phase_angle) / norm
    imag_rows = -window[None, :] * jnp.sin(phase_angle) / norm
    return jnp.concatenate([real_rows, imag_rows], axis=0).astype(jnp.bfloat16)


def transform_blocks(dft_table, snapshots, freq_count, halves):
    local_blocks = snapshots.shape[0] // NT
    points = snapshots.shape[1] // halves
    table_view = dft_table.reshape(2, freq_count, NT).transpose(1, 0, 2)
    chooser = jnp.eye(local_blocks, dtype=dft_table.dtype)
    halver = jnp.eye(halves, dtype=dft_table.dtype)
    lifted = (
        table_view[:, None, :, None, None, None, :]
        * halver[None, :, None, None, :, None, None]
        * chooser[None, None, None, :, None, :, None]
    )
    lifted = lifted.reshape(freq_count * halves * 2 * local_blocks, halves * local_blocks * NT)
    stacked = jnp.concatenate([snapshots[:, h * points:(h + 1) * points] for h in range(halves)], axis=0)
    return jnp.dot(lifted, stacked, preferred_element_type=jnp.float32)


def split_pair(value):
    rounded = lax.reduce_precision(value, exponent_bits=8, mantissa_bits=7)
    return rounded.astype(jnp.bfloat16), (value - rounded).astype(jnp.bfloat16)


NT_DIMS = (((1,), (1,)), ((), ()))


def gram_kernel(group, x_ref, w_ref, o_ref):
    @pl.when(pl.program_id(0) == 0)
    def _():
        o_ref[...] = jnp.zeros_like(o_ref)

    x = x_ref[...]
    x_hi, x_lo = split_pair(x)
    odd = lax.broadcasted_iota(jnp.int32, x.shape, 0) // group % 2 == 1
    row_weights = jnp.where(odd, w_ref[1:2, :], w_ref[0:1, :])
    y_hi, y_lo = split_pair(x * row_weights)
    acc = lax.dot_general(x_hi, y_hi, NT_DIMS, preferred_element_type=jnp.float32)
    acc += lax.dot_general(x_lo, y_hi, NT_DIMS, preferred_element_type=jnp.float32)
    acc += lax.dot_general(x_hi, y_lo, NT_DIMS, preferred_element_type=jnp.float32)
    o_ref[...] += acc


def gram_call(values, weights, chunk, group):
    rows, points = values.shape
    return pl.pallas_call(
        functools.partial(gram_kernel, group),
        grid=(points // chunk,),
        in_specs=[
            pl.BlockSpec((rows, chunk), lambda k: (0, k)),
            pl.BlockSpec((2, chunk), lambda k: (0, k)),
        ],
        compiler_params=pltpu.CompilerParams(allow_input_fusion=[True, False]),
        out_specs=pl.BlockSpec((rows, rows), lambda k: (0, 0)),
        out_shape=jax.ShapeDtypeStruct((rows, rows), jnp.float32),
        cost_estimate=pl.CostEstimate(
            flops=6 * rows * rows * points, transcendentals=0, bytes_accessed=4 * rows * points
        ),
    )(values, weights.reshape(2, points))


def mode_kernel(c_hi_ref, c_lo_ref, x_ref, o_ref):
    x_hi, x_lo = split_pair(x_ref[...])
    c_hi = c_hi_ref[...]
    acc = jnp.dot(c_hi, x_hi, preferred_element_type=jnp.float32)
    acc += jnp.dot(c_lo_ref[...], x_hi, preferred_element_type=jnp.float32)
    acc += jnp.dot(c_hi, x_lo, preferred_element_type=jnp.float32)
    o_ref[...] = acc.astype(o_ref.dtype)


def mode_call(coeff_halves, values, chunk):
    halves, out_rows, rows = coeff_halves.shape
    points = values.shape[1]
    steps = points // chunk
    c_hi, c_lo = split_pair(coeff_halves)
    return pl.pallas_call(
        mode_kernel,
        grid=(steps, halves),
        in_specs=[
            pl.BlockSpec((None, out_rows, rows), lambda k, h: (h, 0, 0)),
            pl.BlockSpec((None, out_rows, rows), lambda k, h: (h, 0, 0)),
            pl.BlockSpec((rows, chunk), lambda k, h: (0, k)),
        ],
        out_specs=pl.BlockSpec((out_rows, chunk), lambda k, h: (0, h * steps + k)),
        out_shape=jax.ShapeDtypeStruct((out_rows, halves * points), jnp.bfloat16),
        compiler_params=pltpu.CompilerParams(allow_input_fusion=[False, False, True]),
        cost_estimate=pl.CostEstimate(
            flops=6 * out_rows * rows * points * halves,
            transcendentals=0,
            bytes_accessed=4 * rows * points * halves + 2 * out_rows * points * halves,
        ),
    )(c_hi, c_lo, values)


def butterfly_sum(value, axis, size):
    step = 1
    while step < size:
        pairs = [(i, i ^ step) for i in range(size)]
        value = value + lax.ppermute(value, axis, pairs)
        step *= 2
    return value


def inverse_root(embedded):
    size_two = embedded.shape[0]
    frobenius = jnp.sqrt(jnp.sum(embedded * embedded) + 1e-06)
    identity = jnp.eye(size_two, dtype=jnp.float32)
    current = embedded / frobenius
    factor = 1.5 * identity - 0.5 * current
    current = jnp.dot(current, factor, precision=HIGH)
    result = factor
    for sweep in range(1, NS_STEPS):
        factor = 1.5 * identity - 0.5 * jnp.dot(result, current, precision=HIGH)
        current = jnp.dot(current, factor, precision=HIGH)
        result = jnp.dot(factor, result, precision=HIGH)
    return result


def shards(data, weights, freqs, n_keep):
    tm_count = lax.axis_size("tm")
    space_count = lax.axis_size("space")
    freq_count = freqs.shape[0]
    points_here = data.shape[1]
    total_points = points_here * space_count
    local_blocks = data.shape[0] // NT
    block_count = local_blocks * tm_count
    rows = 2 * block_count

    dft_table = spectra_table(freqs)
    halves = 2
    spectra = transform_blocks(dft_table, data, freq_count, halves)
    sent = (spectra * LINK_SCALE).astype(jnp.float16)
    received = lax.all_to_all(sent, "tm", split_axis=0, concat_axis=0, tiled=True)
    values = received.astype(jnp.float32)
    recv_rows = received.shape[0]

    square = gram_call(values, weights, 2048, 2 * local_blocks) * (1.0 / (LINK_SCALE * LINK_SCALE * total_points))
    natural = jnp.arange(rows, dtype=jnp.int32)
    part, block = natural // block_count, natural % block_count
    group = 2 * local_blocks
    home = (block // local_blocks) * (group * halves) + part * local_blocks + block % local_blocks
    recv_index = jnp.arange(recv_rows, dtype=jnp.int32)
    pick = [(recv_index[None, :] == (home + h * group)[:, None]).astype(jnp.float32) for h in range(halves)]
    row_half = recv_index // group % halves
    same_half = row_half[:, None] == row_half[None, :]
    either = pick[0] + pick[1]
    square = jnp.where(same_half, square, jnp.zeros_like(square))
    square = jnp.dot(jnp.dot(either, square, precision=HIGH), either.T, precision=HIGH)
    g_one = square[:block_count, :block_count] + square[block_count:, block_count:]
    g_two = square[:block_count, block_count:] - square[block_count:, :block_count]
    lower = jnp.arange(block_count)[:, None] > jnp.arange(block_count)[None, :]
    packed = jnp.where(lower, g_two, g_one)
    rows_half = block_count // 2
    packed = jnp.concatenate([packed[:rows_half], packed[rows_half:]], axis=1)
    spread = jnp.broadcast_to(packed[None], (space_count,) + packed.shape)
    partials = lax.all_to_all(spread, "space", split_axis=0, concat_axis=0, tiled=True)
    total = partials[0]
    for source in range(1, space_count):
        total = total + partials[source]
    total = jnp.concatenate([total[:, :block_count], total[:, block_count:]], axis=0)
    flipped = lax.dot_general(
        jnp.eye(block_count, dtype=jnp.float32), total, NT_DIMS, precision=HIGH
    )
    above = jnp.arange(block_count)[:, None] < jnp.arange(block_count)[None, :]
    g_one = jnp.where(lower, flipped, total)
    g_two = jnp.where(lower, total, jnp.where(above, -flipped, jnp.zeros_like(total)))

    embedded = jnp.concatenate(
        [jnp.concatenate([g_one, -g_two], axis=1), jnp.concatenate([g_two, g_one], axis=1)], axis=0
    )
    inv_root = inverse_root(embedded)
    z_top = inv_root[:block_count, :block_count]
    z_low = inv_root[block_count:, :block_count]
    coeff = jnp.concatenate(
        [jnp.concatenate([z_top.T, -z_low.T], axis=1), jnp.concatenate([z_low.T, z_top.T], axis=1)],
        axis=0,
    )
    kept_count = lax.dynamic_slice_in_dim(n_keep, lax.axis_index("tm"), 1)
    kept_rows = jnp.arange(rows, dtype=jnp.int32) % block_count < kept_count
    coeff = jnp.where(kept_rows[:, None], coeff, jnp.zeros_like(coeff)) * (1.0 / LINK_SCALE)
    coeff_halves = jnp.stack([jnp.dot(coeff, p, precision=HIGH) for p in pick])
    mode_field = mode_call(coeff_halves, values, 1024).reshape(1, 2, block_count, points_here)
    energy = (jnp.trace(g_one) / block_count).reshape(1)
    return (mode_field, energy)


def solution(mesh):
    placed = (P("tm", "space"), P("space"), P(), P())
    return jax.shard_map(
        shards,
        mesh=mesh,
        in_specs=placed,
        out_specs=(P("tm", None, None, "space"), P("tm")),
        check_vma=False,
    )
```
